512 devices in a mesh: seq: 64 (over x, z), head: 8 (over y, core).
Axes of the slice: x: 4, y: 4, z: 16, core: 2. Of those that a mesh axis runs over, the one named last changes fastest.
Arguments:
- tokens: bfloat16 [16384, 4096], P('seq', 'head'), may hold values from -40 to 40
- queries: bfloat16 [16384, 4096], P('seq', 'head'), may hold values from -6 to 6
- key_rows: bfloat16 [16384, 4096], P('seq', 'head'), may hold values from -6 to 6
- values: bfloat16 [16384, 4096], P('seq', 'head'), may hold values from -6 to 6
- log_decay: float32 [32, 16384], P('head', 'seq'), may hold values from -1 to 0
- head_gain: float32 [4096], P('head'), may hold values from 0.5 to 1.5
- expert_gain: float32 [4096], P('head'), may hold values from 0.5 to 1.5
- route_ids: int32 [16384, 2], P('seq'), may hold values from 0 to 31, all different within a row; in each aligned block of 256 rows (0 to 255, 256 to 511, ...) at most 20 rows name the same one
- route_weight: float32 [16384, 2], P('seq'), may hold values from 0.2 to 1
- expert_in: bfloat16 [64, 4096, 1408], P('seq', 'head'), may hold values from -0.09375 to 0.09375
- expert_out: bfloat16 [64, 704, 4096], P('seq', None, 'head'), may hold values from -0.15625 to 0.15625
Outputs:
- mixed: bfloat16 [16384, 4096], P('seq', 'head')
The draws below stay inside these ranges and needn't reach their ends.
Inputs may be any that keep to these rules, and one draw needn't show every extreme that they name: `route_ids`: within the rows of one device (aligned blocks of 256 tokens) no expert is named by more than 20 tokens, a bound that some block reaches; a token's two experts differ.
All inputs are finite; a program needn't handle non-finite values.
Results may differ from the reference program's by a relative error of at most 0.015.
Values may be sent and summed in bfloat16 or wider, within the bound.
No kernel may reach another device: no remote copies, remote signals or barrier semaphores. Data moves between devices by JAX's collectives and lax.ppermute only.
A program may use at most 64 MiB of HBM per device.

```python
import math
import jax
import jax.numpy as jnp
import numpy as np
from jax import lax

ATTENDER_COUNT = 32
HD = 128
D = 4096
EXPERTS = 32
HID = 1408
TOP = 2
TOK_DEV = 256
SPAN_LENGTH = 16384
CAP = 20
HSPLIT = 2
HB = 704
EB = 64
N_SEQ = 64
N_HEAD = 8


def draw_tokens(key, part):
    lookup_projection_array = jax.random.split(key, 1)
    column = jnp.arange(D, dtype=jnp.float32)[None, :] / D
    base = jnp.clip(jax.random.normal(lookup_projection_array[0], (SPAN_LENGTH, D), jnp.float32), -6.0, 6.0)
    result = base * jnp.exp(jnp.log(3.0) * 0.5 * (column - 0.5))
    return result.astype(jnp.bfloat16)


def draw_log_decay(key, part):
    lookup_projection_array = jax.random.split(key, 7)
    position = jnp.arange(SPAN_LENGTH, dtype=jnp.float32)[None, :]
    fast_share = 0.5
    fast = (jax.random.uniform(lookup_projection_array[0], (ATTENDER_COUNT, 1), jnp.float32) < fast_share).astype(jnp.float32)
    slow_rate = jnp.exp(jax.random.uniform(lookup_projection_array[1], (ATTENDER_COUNT, 1), jnp.float32, jnp.log(0.1), jnp.log(0.6))) / SPAN_LENGTH
    fast_rate = jnp.exp(jax.random.uniform(lookup_projection_array[2], (ATTENDER_COUNT, 1), jnp.float32, jnp.log(1.0 / 50.0), jnp.log(1.0 / 30.0)))
    forget_factor = fast * fast_rate + (1.0 - fast) * slow_rate
    phase = jax.random.uniform(lookup_projection_array[3], (ATTENDER_COUNT, 1), jnp.float32, 0.0, 6.2832)
    periodic_sinusoid = jnp.exp(0.7 * jnp.sin(6.2832 * 3.0 * position / SPAN_LENGTH + phase))
    jagged_perturbation = jax.random.uniform(lookup_projection_array[4], (ATTENDER_COUNT, SPAN_LENGTH), jnp.float32, 0.5, 1.5)
    sudden_jolt = (jax.random.uniform(lookup_projection_array[5], (ATTENDER_COUNT, SPAN_LENGTH), jnp.float32) < 1.5 / SPAN_LENGTH).astype(jnp.float32)
    fitting_objective = jnp.log(jax.random.uniform(lookup_projection_array[6], (ATTENDER_COUNT, SPAN_LENGTH), jnp.float32, 0.5, 0.8))
    return (-forget_factor * jagged_perturbation * periodic_sinusoid + sudden_jolt * fitting_objective).astype(jnp.float32)


def level_of(stream_key, dims, shards, low, high):
    level = 1.0
    for dim, parts in shards:
        steps = jax.random.uniform(jax.random.fold_in(jax.random.fold_in(stream_key, 6), dim), (parts,), jnp.float32, low / len(shards), high / len(shards))
        level = level * jnp.repeat(jnp.exp(steps), dims[dim] // parts).reshape((-1,) + (1,) * (len(dims) - 1 - dim))
    return level


def routed_block(rng, own, number, rows, amount, top, most, skew):
    ranking = jax.random.permutation(rng, amount)
    packed, usual = load_shares(amount, rows * top, most, skew, True), load_shares(amount, rows * top, most, skew, False)
    places = jnp.arange(amount)

    def named(tallies, offset_by):
        used = int((tallies > 0).sum())
        fixed = max(1, used // 4)
        passed = fixed + (places - fixed + offset_by * (used - fixed)) % max(1, amount - fixed)
        return jnp.zeros((amount,), jnp.int32).at[ranking[jnp.where(places < fixed, places, passed)]].set(jnp.asarray(tallies, jnp.int32))

    tallies = jnp.where(number % 4 == 0, named(packed, number // 4), named(usual, number - number // 4 - 1))
    mixed = jax.random.permutation(jax.random.fold_in(own, 3), amount)
    giver, receiver = mixed[0:amount // 2 * 2:2], mixed[1:amount // 2 * 2:2]
    margin = jnp.minimum(tallies[giver] - 1, most - tallies[receiver]) // 2
    margin = jnp.where((giver == ranking[0]) | (receiver == ranking[0]) | (tallies[receiver] == 0), 0, jnp.maximum(margin, 0))
    passed = jax.random.randint(jax.random.fold_in(own, 4), (amount // 2,), 0, 1 << 20) % (margin + 1)
    tallies = tallies.at[giver].add(-passed).at[receiver].add(passed)
    members = jnp.searchsorted(jnp.cumsum(tallies), jnp.arange(rows * top), side="right").astype(jnp.int32)
    grid = members.reshape(top, rows).T
    grid = grid[jax.random.permutation(jax.random.fold_in(own, 1), rows)]
    offset_by = jax.random.randint(jax.random.fold_in(own, 2), (rows, 1), 0, top)
    return jnp.take_along_axis(grid, (jnp.arange(top)[None, :] + offset_by) % top, axis=1)


def load_shares(count, total, reach, slope, full):
    weights = [(1 << 20) // math.isqrt(rank ** slope) + 1 for rank in range(1, count + 1)]
    largest = reach if full else min(reach, max(-(-total // count), total * weights[0] // sum(weights)))
    least = 1 if total - largest >= count - 1 else 0
    counts, rest = [largest] + [least] * (count - 1), total - largest - least * (count - 1)
    while rest > 0:
        free = [i for i in range(1, count) if counts[i] < largest] or [i for i in range(1, count) if counts[i] < reach]
        mass, budget = sum([weights[i] for i in free]), rest
        for i in free:
            more = min(reach - counts[i], max(1, budget * weights[i] // mass), rest)
            counts[i] = counts[i] + more
            rest = rest - more
    return np.array(counts)


def noise(rng, shape, scale, limit, pieces=(), kind=jnp.bfloat16):
    values = jax.random.normal(rng, shape, jnp.float32) * scale
    if len(pieces) > 0:
        values = level_of(rng, shape, pieces, -0.22, 0.18) * values
    return jnp.clip(values, min=-limit, max=limit).astype(kind)


def setup_inputs(seed: int = 0) -> dict:
    keys = jax.random.split(jax.random.key(seed), 12)
    tokens = draw_tokens(jax.random.fold_in(keys[11], 71), 0)
    queries = noise(keys[1], (SPAN_LENGTH, D), 1.0, 6.0, ((0, 64), (1, 8)))
    key_rows = noise(keys[2], (SPAN_LENGTH, D), 1.0, 6.0, ((0, 64), (1, 8)))
    values = noise(keys[3], (SPAN_LENGTH, D), 1.0, 6.0, ((0, 64), (1, 8)))
    log_decay = draw_log_decay(jax.random.fold_in(keys[11], 71), 0)
    head_gain = jnp.clip(1.0 + 0.1 * jax.random.normal(keys[5], (D,), jnp.float32), 0.5, 1.5)
    expert_gain = jnp.clip(1.0 + 0.1 * jax.random.normal(keys[6], (D,), jnp.float32), 0.5, 1.5)
    route_ids_keys = jax.random.split(jax.random.fold_in(keys[7], 1), SPAN_LENGTH // TOK_DEV)
    route_ids_turns = jax.random.permutation(jax.random.fold_in(keys[7], 3), SPAN_LENGTH // TOK_DEV)
    route_ids = jax.vmap(lambda own, number: routed_block(jax.random.fold_in(keys[7], 2), own, number, TOK_DEV, EXPERTS, TOP, CAP, 1))(route_ids_keys, route_ids_turns).reshape((SPAN_LENGTH, TOP))
    route_weight = jnp.clip(0.2 + 0.8 * jax.random.uniform(keys[8], (SPAN_LENGTH, TOP), jnp.float32) ** level_of(keys[8], (SPAN_LENGTH, TOP), ((0, 64),), -0.2, 0.2), 0.2, 1.0)
    expert_in = noise(keys[9], (EB, D, 2 * HB), D ** -0.5, 0.09375, ((0, 64), (1, 8)))
    expert_out = noise(keys[10], (EB, HB, D), HID ** -0.5, 0.15625, ((0, 64), (2, 8)))
    return dict(tokens=tokens, queries=queries, key_rows=key_rows, values=values, log_decay=log_decay, head_gain=head_gain, expert_gain=expert_gain, route_ids=route_ids, route_weight=route_weight, expert_in=expert_in, expert_out=expert_out)


EPSILON = 1e-06

def attention_blocks(queries, key_rows, values, log_decay):
    score_scale = HD ** (-0.5)
    query_blocks = queries.reshape(N_SEQ, TOK_DEV, ATTENDER_COUNT, HD).astype(jnp.float32)
    key_blocks = key_rows.reshape(N_SEQ, TOK_DEV, ATTENDER_COUNT, HD).astype(jnp.float32)
    value_blocks = values.reshape(N_SEQ, TOK_DEV, ATTENDER_COUNT, HD).astype(jnp.float32)
    decay_blocks = jnp.transpose(log_decay.reshape(ATTENDER_COUNT, N_SEQ, TOK_DEV), (1, 0, 2))
    causal = jnp.arange(TOK_DEV)[:, None] >= jnp.arange(TOK_DEV)[None, :]

    def advance(state, inputs):
        query_heads, key_heads, value_heads, decay_now = inputs
        cumulative = jnp.cumsum(decay_now, axis=1)
        scores = jnp.einsum('thd,shd->hts', query_heads, key_heads, precision=lax.Precision.HIGHEST) * score_scale
        spread = cumulative[:, :, None] - cumulative[:, None, :]
        mixing = jnp.where(causal[None], scores * jnp.exp(jnp.where(causal[None], spread, 0.0)), 0.0)
        mixing = lax.optimization_barrier(mixing.astype(jnp.bfloat16)).astype(jnp.float32)
        inside = jnp.einsum('hts,shd->thd', mixing, value_heads, precision=lax.Precision.HIGHEST)
        to_end = jnp.exp(cumulative[:, -1:] - cumulative)
        carried_keys = key_heads * to_end.T[:, :, None]
        carried_keys = lax.optimization_barrier(carried_keys.astype(jnp.bfloat16)).astype(jnp.float32)
        block_state = jnp.einsum('shd,she->hde', carried_keys, value_heads, precision=lax.Precision.HIGHEST)
        from_before = jnp.einsum('thd,hde->the', query_heads, state, precision=lax.Precision.HIGHEST)
        attended = inside + from_before * (jnp.exp(cumulative).T[:, :, None] * score_scale)
        new_state = jnp.exp(cumulative[:, -1])[:, None, None] * state + block_state
        return (new_state, attended)
    start = jnp.zeros((ATTENDER_COUNT, HD, HD), jnp.float32)
    final_state, attended = lax.scan(advance, start, (query_blocks, key_blocks, value_blocks, decay_blocks))
    return attended.reshape(SPAN_LENGTH, ATTENDER_COUNT, HD)

def reference(tokens, queries, key_rows, values, log_decay, head_gain, expert_gain, route_ids, route_weight, expert_in, expert_out):
    attended = attention_blocks(queries, key_rows, values, log_decay)
    head_rms = lax.rsqrt(lax.optimization_barrier(jnp.mean(attended * attended, axis=2, keepdims=True)) + EPSILON)
    normed_heads = (attended * head_rms).reshape(SPAN_LENGTH, D)
    hidden_state = (tokens.astype(jnp.float32) + normed_heads * head_gain).astype(jnp.bfloat16)
    hidden_wide = hidden_state.astype(jnp.float32)
    mean_square = lax.optimization_barrier(jnp.mean(hidden_wide * hidden_wide, axis=1))
    expert_input = (hidden_wide * lax.rsqrt(mean_square + EPSILON)[:, None] * expert_gain).astype(jnp.bfloat16)
    flat_ids = route_ids.reshape(N_SEQ, TOK_DEV * TOP)
    chosen = (flat_ids[:, :, None] == jnp.arange(EXPERTS, dtype=jnp.int32)[None, None, :]).astype(jnp.int32)
    before = jnp.cumsum(chosen, axis=1) - chosen
    slot_index = lax.optimization_barrier(jnp.sum(before * chosen, axis=2)).astype(jnp.int32)
    position = (flat_ids * CAP + slot_index).astype(jnp.int32)
    block_rows = jnp.arange(N_SEQ, dtype=jnp.int32)[:, None]
    token_global = (jnp.arange(TOK_DEV * TOP, dtype=jnp.int32)[None, :] // TOP + block_rows * TOK_DEV).astype(jnp.int32)
    token_at = jnp.zeros((N_SEQ, EXPERTS * CAP), jnp.int32).at[block_rows, position].set(token_global)
    weight_at = jnp.zeros((N_SEQ, EXPERTS * CAP), jnp.float32).at[block_rows, position].set(route_weight.reshape(N_SEQ, TOK_DEV * TOP))
    slot_rows = N_SEQ * CAP
    group_width = D // N_HEAD

    def expert_step(total, expert):
        start = (expert * CAP).astype(jnp.int32)
        tokens_here = lax.dynamic_slice_in_dim(token_at, start, CAP, 1).reshape(slot_rows)
        weights_here = lax.dynamic_slice_in_dim(weight_at, start, CAP, 1).reshape(slot_rows)
        gathered = expert_input[tokens_here].reshape(slot_rows, N_HEAD, group_width).astype(jnp.float32)
        output = jnp.zeros((slot_rows, D), jnp.float32)
        for part_index in range(HSPLIT):
            block_index = (expert * HSPLIT + part_index).astype(jnp.int32)
            weight_in = lax.dynamic_index_in_dim(expert_in, block_index, 0, keepdims=False)
            weight_in = weight_in.reshape(N_HEAD, group_width, 2 * HB).astype(jnp.float32)
            partial_sums = jnp.einsum('rgd,gdh->rgh', gathered, weight_in, precision=lax.Precision.HIGHEST)
            rounded = lax.optimization_barrier(partial_sums.astype(jnp.bfloat16)).astype(jnp.float32)
            gate_up = lax.optimization_barrier(jnp.sum(rounded, axis=1))
            activated = (jax.nn.silu(gate_up[:, :HB]) * gate_up[:, HB:]).astype(jnp.bfloat16)
            weight_out = lax.dynamic_index_in_dim(expert_out, block_index, 0, keepdims=False)
            expert_part = jnp.dot(activated, weight_out, preferred_element_type=jnp.float32).astype(jnp.bfloat16)
            output = output + expert_part.astype(jnp.float32)
        return (total.at[tokens_here].add(output * weights_here[:, None]), None)
    expert_mix, unused = lax.scan(expert_step, jnp.zeros((SPAN_LENGTH, D), jnp.float32), jnp.arange(EXPERTS, dtype=jnp.int32))
    return (hidden_wide + expert_mix).astype(jnp.bfloat16)
```

```python
import jax
import jax.numpy as jnp
from jax import lax
from jax.sharding import PartitionSpec as P

D = 4096
EXPERTS = 32
CAP = 20


EPSILON = 1e-06


def exclusive_scan(decay, state, axis):
    place = lax.axis_index(axis)
    count = lax.axis_size(axis)
    heads, rows, cols = state.shape
    own = jnp.concatenate(
        [state, jnp.broadcast_to(decay[:, None, None], (heads, 1, cols))], axis=1
    )
    window = own
    before_decay = jnp.ones_like(decay)
    before_state = jnp.zeros_like(state)
    shift = 1
    while shift < count:
        pairs = [(j, j + shift) for j in range(count - shift)]
        got = lax.ppermute(window, axis, pairs)
        valid = place >= shift
        got_state = got[:, :rows, :]
        got_decay = jnp.where(valid, got[:, rows, 0], 1.0)
        before_state = before_decay[:, None, None] * got_state + before_state
        before_decay = before_decay * got_decay
        window_decay = window[:, rows, 0]
        window_state = window_decay[:, None, None] * got_state + window[:, :rows, :]
        window_decay = window_decay * got_decay
        window = jnp.concatenate(
            [window_state, jnp.broadcast_to(window_decay[:, None, None], (heads, 1, cols))],
            axis=1,
        )
        shift *= 2
    return before_state


def per_device(
    tokens,
    queries,
    key_rows,
    values,
    log_decay,
    head_gain,
    expert_gain,
    route_ids,
    route_weight,
    expert_in,
    expert_out,
):
    length = tokens.shape[0]
    local_width = tokens.shape[1]
    heads_here = log_decay.shape[0]
    head_size = queries.shape[1] // heads_here
    score_scale = head_size ** (-0.5)
    query_heads = queries.reshape(length, heads_here, head_size)
    key_heads = key_rows.reshape(length, heads_here, head_size)
    value_heads = values.reshape(length, heads_here, head_size)
    cumulative = jnp.cumsum(log_decay, axis=1)
    causal = (jnp.arange(length)[:, None] >= jnp.arange(length)[None, :])[None]
    scores = (
        jnp.einsum("thd,shd->hts", query_heads, key_heads, preferred_element_type=jnp.float32)
        * score_scale
    )
    spread = cumulative[:, :, None] - cumulative[:, None, :]
    mixing = jnp.where(causal, scores * jnp.exp(jnp.where(causal, spread, 0.0)), 0.0).astype(
        jnp.bfloat16
    )
    inside = jnp.einsum("hts,shd->thd", mixing, value_heads, preferred_element_type=jnp.float32)
    to_end = jnp.exp(cumulative[:, -1:] - cumulative)
    carried_keys = (key_heads.astype(jnp.float32) * to_end.T[:, :, None]).astype(jnp.bfloat16)
    block_state = jnp.einsum(
        "shd,she->hde", carried_keys, value_heads, preferred_element_type=jnp.float32
    )
    block_decay = jnp.exp(cumulative[:, -1])
    entering = exclusive_scan(block_decay, block_state, "seq")
    from_before = jnp.einsum(
        "thd,hde->the",
        query_heads.astype(jnp.float32),
        entering,
        precision=lax.Precision.HIGHEST,
        preferred_element_type=jnp.float32,
    )
    attended = inside + from_before * (jnp.exp(cumulative).T[:, :, None] * score_scale)
    head_rms = lax.rsqrt(jnp.mean(attended * attended, axis=2, keepdims=True) + EPSILON)
    normed_heads = (attended * head_rms).reshape(length, local_width)
    hidden_state = (tokens.astype(jnp.float32) + normed_heads * head_gain).astype(jnp.bfloat16)
    hidden_wide = hidden_state.astype(jnp.float32)
    local_squares = jnp.sum(hidden_wide * hidden_wide, axis=1)
    total_squares = lax.psum(local_squares, "head")
    inverse_rms = lax.rsqrt(total_squares / D + EPSILON)
    expert_input = (hidden_wide * inverse_rms[:, None] * expert_gain).astype(jnp.bfloat16)
    capacity = CAP
    expert_count = EXPERTS
    flat_ids = route_ids.reshape(-1)
    pair_count = flat_ids.shape[0]
    chosen = (flat_ids[:, None] == jnp.arange(expert_count)[None, :]).astype(jnp.float32)
    strictly_before = (jnp.arange(pair_count)[:, None] > jnp.arange(pair_count)[None, :]).astype(
        jnp.float32
    )
    earlier_counts = jnp.dot(
        strictly_before, chosen, precision=lax.Precision.HIGHEST, preferred_element_type=jnp.float32
    )
    slot_index = jnp.sum(earlier_counts * chosen, axis=1).astype(jnp.int32)
    position = (flat_ids * capacity + slot_index).reshape(length, route_ids.shape[1])
    slot_ids = jnp.arange(expert_count * capacity, dtype=jnp.int32)
    picks = position[None, :, :] == slot_ids[:, None, None]
    dispatch_matrix = jnp.any(picks, axis=2).astype(jnp.bfloat16)
    send_rows = jnp.dot(dispatch_matrix, expert_input, preferred_element_type=jnp.float32).astype(
        jnp.bfloat16
    )
    hidden_split = expert_in.shape[0] * lax.axis_size("seq") // expert_count
    send_buffer = jnp.repeat(
        send_rows.reshape(expert_count, 1, capacity, local_width), hidden_split, axis=0
    )
    block_units = expert_out.shape[1]
    arrived = lax.all_to_all(send_buffer, "seq", split_axis=0, concat_axis=1, tiled=True)
    blocks_here, sources, item_count, feature_count = arrived.shape
    flat_rows = arrived.reshape(blocks_here, sources * item_count, feature_count)
    partial_sums = jnp.einsum(
        "erd,edh->erh", flat_rows, expert_in, preferred_element_type=jnp.float32
    )
    partial_sums = partial_sums.reshape(blocks_here, sources, item_count, 2, block_units)
    gate_up = lax.psum(partial_sums.astype(jnp.bfloat16), "head").astype(jnp.float32)
    activated = (jax.nn.silu(gate_up[:, :, :, 0]) * gate_up[:, :, :, 1]).astype(jnp.bfloat16)
    activated = activated.reshape(blocks_here, sources * item_count, block_units)
    produced = jnp.einsum(
        "erh,ehd->erd", activated, expert_out, preferred_element_type=jnp.float32
    ).astype(jnp.bfloat16)
    computed = produced.reshape(blocks_here, sources, item_count, feature_count)
    returned = lax.all_to_all(computed, "seq", split_axis=1, concat_axis=0, tiled=True)
    merged = jnp.sum(
        returned.reshape(expert_count, hidden_split, capacity, local_width).astype(jnp.float32),
        axis=1,
    )
    merged = merged.reshape(expert_count * capacity, local_width)
    slot_rows = merged[position]
    expert_mix = jnp.sum(slot_rows * route_weight[:, :, None], axis=1)
    return (hidden_wide + expert_mix).astype(jnp.bfloat16)


def solution(mesh):
    return jax.shard_map(
        per_device,
        mesh=mesh,
        in_specs=(
            P("seq", "head"),
            P("seq", "head"),
            P("seq", "head"),
            P("seq", "head"),
            P("head", "seq"),
            P("head"),
            P("head"),
            P("seq", None),
            P("seq", None),
            P("seq", "head", None),
            P("seq", None, "head"),
        ),
        out_specs=P("seq", "head"),
        check_vma=False,
    )
```

```python
import jax
import jax.numpy as jnp
from jax import lax
from jax.sharding import PartitionSpec as P

D = 4096
EXPERTS = 32
CAP = 20
CHUNKS = ((0, 10), (10, 20))


EPSILON = 1e-06


def exclusive_scan(decay, state, axis):
    place = lax.axis_index(axis)
    count = lax.axis_size(axis)
    heads, rows, cols = state.shape
    own = jnp.concatenate(
        [state, jnp.broadcast_to(decay[:, None, None], (heads, 1, cols))], axis=1
    )
    window = own
    before_decay = jnp.ones_like(decay)
    before_state = jnp.zeros_like(state)
    shift = 1
    while shift < count:
        pairs = [(j, j + shift) for j in range(count - shift)]
        got = lax.ppermute(window, axis, pairs)
        valid = place >= shift
        got_state = got[:, :rows, :]
        got_decay = jnp.where(valid, got[:, rows, 0], 1.0)
        before_state = before_decay[:, None, None] * got_state + before_state
        before_decay = before_decay * got_decay
        window_decay = window[:, rows, 0]
        window_state = window_decay[:, None, None] * got_state + window[:, :rows, :]
        window_decay = window_decay * got_decay
        window = jnp.concatenate(
            [window_state, jnp.broadcast_to(window_decay[:, None, None], (heads, 1, cols))],
            axis=1,
        )
        shift *= 2
    return before_state


def per_device(
    tokens,
    queries,
    key_rows,
    values,
    log_decay,
    head_gain,
    expert_gain,
    route_ids,
    route_weight,
    expert_in,
    expert_out,
):
    length = tokens.shape[0]
    local_width = tokens.shape[1]
    heads_here = log_decay.shape[0]
    head_size = queries.shape[1] // heads_here
    score_scale = head_size ** (-0.5)
    query_heads = queries.reshape(length, heads_here, head_size)
    key_heads = key_rows.reshape(length, heads_here, head_size)
    value_heads = values.reshape(length, heads_here, head_size)
    cumulative = jnp.cumsum(log_decay, axis=1)
    causal = (jnp.arange(length)[:, None] >= jnp.arange(length)[None, :])[None]
    scores = (
        jnp.einsum("thd,shd->hts", query_heads, key_heads, preferred_element_type=jnp.float32)
        * score_scale
    )
    spread = cumulative[:, :, None] - cumulative[:, None, :]
    mixing = jnp.where(causal, scores * jnp.exp(jnp.where(causal, spread, 0.0)), 0.0).astype(
        jnp.bfloat16
    )
    inside = jnp.einsum("hts,shd->thd", mixing, value_heads, preferred_element_type=jnp.float32)
    to_end = jnp.exp(cumulative[:, -1:] - cumulative)
    carried_keys = (key_heads.astype(jnp.float32) * to_end.T[:, :, None]).astype(jnp.bfloat16)
    block_state = jnp.einsum(
        "shd,she->hde", carried_keys, value_heads, preferred_element_type=jnp.float32
    )
    block_decay = jnp.exp(cumulative[:, -1])
    entering = exclusive_scan(block_decay, block_state, "seq")
    from_before = jnp.einsum(
        "thd,hde->the",
        query_heads.astype(jnp.float32),
        entering,
        precision=lax.Precision.HIGHEST,
        preferred_element_type=jnp.float32,
    )
    attended = inside + from_before * (jnp.exp(cumulative).T[:, :, None] * score_scale)
    head_rms = lax.rsqrt(jnp.mean(attended * attended, axis=2, keepdims=True) + EPSILON)
    normed_heads = (attended * head_rms).reshape(length, local_width)
    hidden_state = (tokens.astype(jnp.float32) + normed_heads * head_gain).astype(jnp.bfloat16)
    hidden_wide = hidden_state.astype(jnp.float32)
    local_squares = jnp.sum(hidden_wide * hidden_wide, axis=1)
    total_squares = lax.psum(local_squares, "head")
    inverse_rms = lax.rsqrt(total_squares / D + EPSILON)
    expert_input = (hidden_wide * inverse_rms[:, None] * expert_gain).astype(jnp.bfloat16)
    capacity = CAP
    expert_count = EXPERTS
    flat_ids = route_ids.reshape(-1)
    pair_count = flat_ids.shape[0]
    chosen = (flat_ids[:, None] == jnp.arange(expert_count)[None, :]).astype(jnp.float32)
    strictly_before = (jnp.arange(pair_count)[:, None] > jnp.arange(pair_count)[None, :]).astype(
        jnp.float32
    )
    earlier_counts = jnp.dot(
        strictly_before, chosen, precision=lax.Precision.HIGHEST, preferred_element_type=jnp.float32
    )
    slot_index = jnp.sum(earlier_counts * chosen, axis=1).astype(jnp.int32)
    position = (flat_ids * capacity + slot_index).reshape(length, route_ids.shape[1])
    slot_ids = jnp.arange(expert_count * capacity, dtype=jnp.int32)
    picks = position[None, :, :] == slot_ids[:, None, None]
    dispatch_matrix = jnp.any(picks, axis=2).astype(jnp.bfloat16)
    send_rows = jnp.dot(dispatch_matrix, expert_input, preferred_element_type=jnp.float32).astype(
        jnp.bfloat16
    )
    hidden_split = expert_in.shape[0] * lax.axis_size("seq") // expert_count
    send_buffer = jnp.repeat(
        send_rows.reshape(expert_count, 1, capacity, local_width), hidden_split, axis=0
    )
    block_units = expert_out.shape[1]
    pieces = []
    earlier = None
    for lo, hi in CHUNKS:
        arrived = lax.all_to_all(
            send_buffer[:, :, lo:hi], "seq", split_axis=0, concat_axis=1, tiled=True
        )
        blocks_here, sources, item_count, feature_count = arrived.shape
        flat_rows = arrived.reshape(blocks_here, sources * item_count, feature_count)
        partial_sums = jnp.einsum(
            "erd,edh->erh", flat_rows, expert_in, preferred_element_type=jnp.float32
        )
        partial_sums = partial_sums.reshape(blocks_here, sources, item_count, 2, block_units)
        if earlier is not None:
            partial_sums, earlier = lax.optimization_barrier((partial_sums, earlier))
        gate_up = lax.psum(partial_sums.astype(jnp.bfloat16), "head").astype(jnp.float32)
        earlier = gate_up
        activated = (jax.nn.silu(gate_up[:, :, :, 0]) * gate_up[:, :, :, 1]).astype(jnp.bfloat16)
        activated = activated.reshape(blocks_here, sources * item_count, block_units)
        produced = jnp.einsum(
            "erh,ehd->erd", activated, expert_out, preferred_element_type=jnp.float32
        ).astype(jnp.bfloat16)
        computed = produced.reshape(blocks_here, sources, item_count, feature_count)
        returned = lax.all_to_all(computed, "seq", split_axis=1, concat_axis=0, tiled=True)
        pieces.append(
            jnp.sum(
                returned.reshape(expert_count, hidden_split, item_count, local_width).astype(
                    jnp.float32
                ),
                axis=1,
            )
        )
    merged = jnp.concatenate(pieces, axis=1)
    merged = merged.reshape(expert_count * capacity, local_width)
    slot_rows = merged[position]
    expert_mix = jnp.sum(slot_rows * route_weight[:, :, None], axis=1)
    return (hidden_wide + expert_mix).astype(jnp.bfloat16)


def solution(mesh):
    return jax.shard_map(
        per_device,
        mesh=mesh,
        in_specs=(
            P("seq", "head"),
            P("seq", "head"),
            P("seq", "head"),
            P("seq", "head"),
            P("head", "seq"),
            P("head"),
            P("head"),
            P("seq", None),
            P("seq", None),
            P("seq", "head", None),
            P("seq", None, "head"),
        ),
        out_specs=P("seq", "head"),
        check_vma=False,
    )
```

```python
import jax
import jax.numpy as jnp
from jax import lax
from jax.sharding import PartitionSpec as P

D = 4096
EXPERTS = 32
CAP = 20


EPSILON = 1e-06


def exclusive_scan(decay, state, axis):
    place = lax.axis_index(axis)
    count = lax.axis_size(axis)
    heads, rows, cols = state.shape
    own = jnp.concatenate(
        [state, jnp.broadcast_to(decay[:, None, None], (heads, 1, cols))], axis=1
    )
    window = own
    before_decay = jnp.ones_like(decay)
    before_state = jnp.zeros_like(state)
    shift = 1
    while shift < count:
        pairs = [(j, j + shift) for j in range(count - shift)]
        got = lax.ppermute(window, axis, pairs)
        valid = place >= shift
        got_state = got[:, :rows, :]
        got_decay = jnp.where(valid, got[:, rows, 0], 1.0)
        before_state = before_decay[:, None, None] * got_state + before_state
        before_decay = before_decay * got_decay
        window_decay = window[:, rows, 0]
        window_state = window_decay[:, None, None] * got_state + window[:, :rows, :]
        window_decay = window_decay * got_decay
        window = jnp.concatenate(
            [window_state, jnp.broadcast_to(window_decay[:, None, None], (heads, 1, cols))],
            axis=1,
        )
        shift *= 2
    return before_state


def head_reduce_activate(partial, axis, block_units):
    place = lax.axis_index(axis)
    count = lax.axis_size(axis)
    blocks_here, rows, width = partial.shape
    share = rows // count
    pieces = partial.reshape(blocks_here, count, share, width)
    total = lax.dynamic_index_in_dim(pieces, place, 1, False).astype(jnp.float32)
    for shift in range(1, count):
        target = (place + shift) % count
        outgoing = lax.dynamic_index_in_dim(pieces, target, 1, False)
        pairs = [(j, (j + shift) % count) for j in range(count)]
        total = total + lax.ppermute(outgoing, axis, pairs).astype(jnp.float32)
    gate = total[:, :, :block_units]
    up = total[:, :, block_units:]
    mine = (jax.nn.silu(gate) * up).astype(jnp.bfloat16)
    gathered = [mine]
    for shift in range(1, count):
        pairs = [(j, (j + shift) % count) for j in range(count)]
        gathered.append(lax.ppermute(mine, axis, pairs))
    stacked = jnp.stack(gathered, axis=1)
    origin = (place - jnp.arange(count)) % count
    ordered = jnp.take(stacked, origin, axis=1)
    return ordered.reshape(blocks_here, rows, block_units)


def per_device(
    tokens,
    queries,
    key_rows,
    values,
    log_decay,
    head_gain,
    expert_gain,
    route_ids,
    route_weight,
    expert_in,
    expert_out,
):
    length = tokens.shape[0]
    local_width = tokens.shape[1]
    heads_here = log_decay.shape[0]
    head_size = queries.shape[1] // heads_here
    score_scale = head_size ** (-0.5)
    query_heads = queries.reshape(length, heads_here, head_size)
    key_heads = key_rows.reshape(length, heads_here, head_size)
    value_heads = values.reshape(length, heads_here, head_size)
    cumulative = jnp.cumsum(log_decay, axis=1)
    causal = (jnp.arange(length)[:, None] >= jnp.arange(length)[None, :])[None]
    scores = (
        jnp.einsum("thd,shd->hts", query_heads, key_heads, preferred_element_type=jnp.float32)
        * score_scale
    )
    spread = cumulative[:, :, None] - cumulative[:, None, :]
    mixing = jnp.where(causal, scores * jnp.exp(jnp.where(causal, spread, 0.0)), 0.0).astype(
        jnp.bfloat16
    )
    inside = jnp.einsum("hts,shd->thd", mixing, value_heads, preferred_element_type=jnp.float32)
    to_end = jnp.exp(cumulative[:, -1:] - cumulative)
    carried_keys = (key_heads.astype(jnp.float32) * to_end.T[:, :, None]).astype(jnp.bfloat16)
    block_state = jnp.einsum(
        "shd,she->hde", carried_keys, value_heads, preferred_element_type=jnp.float32
    )
    block_decay = jnp.exp(cumulative[:, -1])
    entering = exclusive_scan(block_decay, block_state, "seq")
    from_before = jnp.einsum(
        "thd,hde->the",
        query_heads.astype(jnp.float32),
        entering,
        precision=lax.Precision.HIGHEST,
        preferred_element_type=jnp.float32,
    )
    attended = inside + from_before * (jnp.exp(cumulative).T[:, :, None] * score_scale)
    head_rms = lax.rsqrt(jnp.mean(attended * attended, axis=2, keepdims=True) + EPSILON)
    normed_heads = (attended * head_rms).reshape(length, local_width)
    hidden_state = (tokens.astype(jnp.float32) + normed_heads * head_gain).astype(jnp.bfloat16)
    hidden_wide = hidden_state.astype(jnp.float32)
    local_squares = jnp.sum(hidden_wide * hidden_wide, axis=1)
    total_squares = lax.psum(local_squares, "head")
    inverse_rms = lax.rsqrt(total_squares / D + EPSILON)
    expert_input = (hidden_wide * inverse_rms[:, None] * expert_gain).astype(jnp.bfloat16)
    capacity = CAP
    expert_count = EXPERTS
    flat_ids = route_ids.reshape(-1)
    pair_count = flat_ids.shape[0]
    chosen = (flat_ids[:, None] == jnp.arange(expert_count)[None, :]).astype(jnp.float32)
    strictly_before = (jnp.arange(pair_count)[:, None] > jnp.arange(pair_count)[None, :]).astype(
        jnp.float32
    )
    earlier_counts = jnp.dot(
        strictly_before, chosen, precision=lax.Precision.HIGHEST, preferred_element_type=jnp.float32
    )
    slot_index = jnp.sum(earlier_counts * chosen, axis=1).astype(jnp.int32)
    position = (flat_ids * capacity + slot_index).reshape(length, route_ids.shape[1])
    slot_ids = jnp.arange(expert_count * capacity, dtype=jnp.int32)
    picks = position[None, :, :] == slot_ids[:, None, None]
    dispatch_matrix = jnp.any(picks, axis=2).astype(jnp.bfloat16)
    send_rows = jnp.dot(dispatch_matrix, expert_input, preferred_element_type=jnp.float32).astype(
        jnp.bfloat16
    )
    hidden_split = expert_in.shape[0] * lax.axis_size("seq") // expert_count
    send_buffer = jnp.repeat(
        send_rows.reshape(expert_count, 1, capacity, local_width), hidden_split, axis=0
    )
    block_units = expert_out.shape[1]
    arrived = lax.all_to_all(send_buffer, "seq", split_axis=0, concat_axis=1, tiled=True)
    blocks_here, sources, item_count, feature_count = arrived.shape
    flat_rows = arrived.reshape(blocks_here, sources * item_count, feature_count)
    partial_sums = jnp.einsum(
        "erd,edh->erh", flat_rows, expert_in, preferred_element_type=jnp.float32
    )
    activated = head_reduce_activate(partial_sums.astype(jnp.bfloat16), "head", block_units)
    produced = jnp.einsum(
        "erh,ehd->erd", activated, expert_out, preferred_element_type=jnp.float32
    ).astype(jnp.bfloat16)
    computed = produced.reshape(blocks_here, sources, item_count, feature_count)
    returned = lax.all_to_all(computed, "seq", split_axis=1, concat_axis=0, tiled=True)
    merged = jnp.sum(
        returned.reshape(expert_count, hidden_split, capacity, local_width).astype(jnp.float32),
        axis=1,
    )
    merged = merged.reshape(expert_count * capacity, local_width)
    slot_rows = merged[position]
    expert_mix = jnp.sum(slot_rows * route_weight[:, :, None], axis=1)
    return (hidden_wide + expert_mix).astype(jnp.bfloat16)


def solution(mesh):
    return jax.shard_map(
        per_device,
        mesh=mesh,
        in_specs=(
            P("seq", "head"),
            P("seq", "head"),
            P("seq", "head"),
            P("seq", "head"),
            P("head", "seq"),
            P("head"),
            P("head"),
            P("seq", None),
            P("seq", None),
            P("seq", "head", None),
            P("seq", None, "head"),
        ),
        out_specs=P("seq", "head"),
        check_vma=False,
    )
```

```python
import jax
import jax.numpy as jnp
from jax import lax
from jax.sharding import PartitionSpec as P

D = 4096
EXPERTS = 32
CAP = 20


EPSILON = 1e-06


def pack_window(decay, state):
    heads, rows, cols = state.shape
    high = decay.astype(jnp.bfloat16)
    low = (decay - high.astype(jnp.float32)).astype(jnp.bfloat16)
    tail = jnp.broadcast_to(jnp.stack([high, low], axis=1)[:, :, None], (heads, 2, cols))
    return jnp.concatenate([state.astype(jnp.bfloat16), tail], axis=1)


def exclusive_scan(decay, state, axis):
    place = lax.axis_index(axis)
    count = lax.axis_size(axis)
    rows = state.shape[1]
    window_decay = decay
    window_state = state
    before_decay = jnp.ones_like(decay)
    before_state = jnp.zeros_like(state)
    shift = 1
    while shift < count:
        pairs = [(j, j + shift) for j in range(count - shift)]
        got = lax.ppermute(pack_window(window_decay, window_state), axis, pairs)
        valid = place >= shift
        got_state = got[:, :rows, :].astype(jnp.float32)
        got_decay = got[:, rows, 0].astype(jnp.float32) + got[:, rows + 1, 0].astype(jnp.float32)
        got_decay = jnp.where(valid, got_decay, 1.0)
        before_state = before_decay[:, None, None] * got_state + before_state
        before_decay = before_decay * got_decay
        window_state = window_decay[:, None, None] * got_state + window_state
        window_decay = window_decay * got_decay
        shift *= 2
    return before_state


def head_reduce_activate(partial, axis, block_units):
    place = lax.axis_index(axis)
    count = lax.axis_size(axis)
    blocks_here, rows, width = partial.shape
    share = rows // count
    pieces = partial.reshape(blocks_here, count, share, width)
    total = lax.dynamic_index_in_dim(pieces, place, 1, False).astype(jnp.float32)
    for shift in range(1, count):
        target = (place + shift) % count
        outgoing = lax.dynamic_index_in_dim(pieces, target, 1, False)
        pairs = [(j, (j + shift) % count) for j in range(count)]
        total = total + lax.ppermute(outgoing, axis, pairs).astype(jnp.float32)
    gate = total[:, :, :block_units]
    up = total[:, :, block_units:]
    mine = (jax.nn.silu(gate) * up).astype(jnp.bfloat16)
    gathered = [mine]
    for shift in range(1, count):
        pairs = [(j, (j + shift) % count) for j in range(count)]
        gathered.append(lax.ppermute(mine, axis, pairs))
    stacked = jnp.stack(gathered, axis=1)
    origin = (place - jnp.arange(count)) % count
    ordered = jnp.take(stacked, origin, axis=1)
    return ordered.reshape(blocks_here, rows, block_units)


def per_device(
    tokens,
    queries,
    key_rows,
    values,
    log_decay,
    head_gain,
    expert_gain,
    route_ids,
    route_weight,
    expert_in,
    expert_out,
):
    length = tokens.shape[0]
    local_width = tokens.shape[1]
    heads_here = log_decay.shape[0]
    head_size = queries.shape[1] // heads_here
    score_scale = head_size ** (-0.5)
    query_heads = queries.reshape(length, heads_here, head_size)
    key_heads = key_rows.reshape(length, heads_here, head_size)
    value_heads = values.reshape(length, heads_here, head_size)
    cumulative = jnp.cumsum(log_decay, axis=1)
    causal = (jnp.arange(length)[:, None] >= jnp.arange(length)[None, :])[None]
    scores = (
        jnp.einsum("thd,shd->hts", query_heads, key_heads, preferred_element_type=jnp.float32)
        * score_scale
    )
    spread = cumulative[:, :, None] - cumulative[:, None, :]
    mixing = jnp.where(causal, scores * jnp.exp(jnp.where(causal, spread, 0.0)), 0.0).astype(
        jnp.bfloat16
    )
    inside = jnp.einsum("hts,shd->thd", mixing, value_heads, preferred_element_type=jnp.float32)
    to_end = jnp.exp(cumulative[:, -1:] - cumulative)
    carried_keys = (key_heads.astype(jnp.float32) * to_end.T[:, :, None]).astype(jnp.bfloat16)
    block_state = jnp.einsum(
        "shd,she->hde", carried_keys, value_heads, preferred_element_type=jnp.float32
    )
    block_decay = jnp.exp(cumulative[:, -1])
    entering = exclusive_scan(block_decay, block_state, "seq")
    from_before = jnp.einsum(
        "thd,hde->the",
        query_heads.astype(jnp.float32),
        entering,
        precision=lax.Precision.HIGHEST,
        preferred_element_type=jnp.float32,
    )
    attended = inside + from_before * (jnp.exp(cumulative).T[:, :, None] * score_scale)
    head_rms = lax.rsqrt(jnp.mean(attended * attended, axis=2, keepdims=True) + EPSILON)
    normed_heads = (attended * head_rms).reshape(length, local_width)
    hidden_state = (tokens.astype(jnp.float32) + normed_heads * head_gain).astype(jnp.bfloat16)
    hidden_wide = hidden_state.astype(jnp.float32)
    local_squares = jnp.sum(hidden_wide * hidden_wide, axis=1)
    total_squares = lax.psum(local_squares, "head")
    inverse_rms = lax.rsqrt(total_squares / D + EPSILON)
    expert_input = (hidden_wide * inverse_rms[:, None] * expert_gain).astype(jnp.bfloat16)
    capacity = CAP
    expert_count = EXPERTS
    flat_ids = route_ids.reshape(-1)
    pair_count = flat_ids.shape[0]
    chosen = (flat_ids[:, None] == jnp.arange(expert_count)[None, :]).astype(jnp.float32)
    strictly_before = (jnp.arange(pair_count)[:, None] > jnp.arange(pair_count)[None, :]).astype(
        jnp.float32
    )
    earlier_counts = jnp.dot(
        strictly_before, chosen, precision=lax.Precision.HIGHEST, preferred_element_type=jnp.float32
    )
    slot_index = jnp.sum(earlier_counts * chosen, axis=1).astype(jnp.int32)
    position = (flat_ids * capacity + slot_index).reshape(length, route_ids.shape[1])
    slot_ids = jnp.arange(expert_count * capacity, dtype=jnp.int32)
    picks = position[None, :, :] == slot_ids[:, None, None]
    dispatch_matrix = jnp.any(picks, axis=2).astype(jnp.bfloat16)
    send_rows = jnp.dot(dispatch_matrix, expert_input, preferred_element_type=jnp.float32).astype(
        jnp.bfloat16
    )
    hidden_split = expert_in.shape[0] * lax.axis_size("seq") // expert_count
    send_buffer = jnp.repeat(
        send_rows.reshape(expert_count, 1, capacity, local_width), hidden_split, axis=0
    )
    block_units = expert_out.shape[1]
    arrived = lax.all_to_all(send_buffer, "seq", split_axis=0, concat_axis=1, tiled=True)
    blocks_here, sources, item_count, feature_count = arrived.shape
    flat_rows = arrived.reshape(blocks_here, sources * item_count, feature_count)
    partial_sums = jnp.einsum(
        "erd,edh->erh", flat_rows, expert_in, preferred_element_type=jnp.float32
    )
    activated = head_reduce_activate(partial_sums.astype(jnp.bfloat16), "head", block_units)
    produced = jnp.einsum(
        "erh,ehd->erd", activated, expert_out, preferred_element_type=jnp.float32
    ).astype(jnp.bfloat16)
    computed = produced.reshape(blocks_here, sources, item_count, feature_count)
    returned = lax.all_to_all(computed, "seq", split_axis=1, concat_axis=0, tiled=True)
    merged = jnp.sum(
        returned.reshape(expert_count, hidden_split, capacity, local_width).astype(jnp.float32),
        axis=1,
    )
    merged = merged.reshape(expert_count * capacity, local_width)
    slot_rows = merged[position]
    expert_mix = jnp.sum(slot_rows * route_weight[:, :, None], axis=1)
    return (hidden_wide + expert_mix).astype(jnp.bfloat16)


def solution(mesh):
    return jax.shard_map(
        per_device,
        mesh=mesh,
        in_specs=(
            P("seq", "head"),
            P("seq", "head"),
            P("seq", "head"),
            P("seq", "head"),
            P("head", "seq"),
            P("head"),
            P("head"),
            P("seq", None),
            P("seq", None),
            P("seq", "head", None),
            P("seq", None, "head"),
        ),
        out_specs=P("seq", "head"),
        check_vma=False,
    )
```

```python
import jax
import jax.numpy as jnp
from jax import lax
from jax.sharding import PartitionSpec as P

D = 4096
EXPERTS = 32
CAP = 20


EPSILON = 1e-06


def pack_window(decay, state):
    heads, rows, cols = state.shape
    high = decay.astype(jnp.bfloat16)
    low = (decay - high.astype(jnp.float32)).astype(jnp.bfloat16)
    tail = jnp.broadcast_to(jnp.stack([high, low], axis=1)[:, :, None], (heads, 2, cols))
    return jnp.concatenate([state.astype(jnp.bfloat16), tail], axis=1)


def exclusive_scan(decay, state, axis):
    place = lax.axis_index(axis)
    count = lax.axis_size(axis)
    rows = state.shape[1]
    window_decay = decay
    window_state = state
    before_decay = jnp.ones_like(decay)
    before_state = jnp.zeros_like(state)
    shift = 1
    while shift < count:
        pairs = [(j, j + shift) for j in range(count - shift)]
        got = lax.ppermute(pack_window(window_decay, window_state), axis, pairs)
        valid = place >= shift
        got_state = got[:, :rows, :].astype(jnp.float32)
        got_decay = got[:, rows, 0].astype(jnp.float32) + got[:, rows + 1, 0].astype(jnp.float32)
        got_decay = jnp.where(valid, got_decay, 1.0)
        before_state = before_decay[:, None, None] * got_state + before_state
        before_decay = before_decay * got_decay
        window_state = window_decay[:, None, None] * got_state + window_state
        window_decay = window_decay * got_decay
        shift *= 2
    return before_state


def head_reduce_activate(partial, axis, block_units):
    place = lax.axis_index(axis)
    count = lax.axis_size(axis)
    chips = count // 2
    core = place % 2
    chip = place // 2
    blocks_here, rows, width = partial.shape
    share = rows // count
    pieces = partial.reshape(blocks_here, chips, 2, share, width)
    sibling = [(j, j ^ 1) for j in range(count)]
    kept = lax.dynamic_index_in_dim(pieces, core, 2, False).astype(jnp.float32)
    handed = lax.dynamic_index_in_dim(pieces, 1 - core, 2, False)
    pair_sum = kept + lax.ppermute(handed, axis, sibling).astype(jnp.float32)
    total = lax.dynamic_index_in_dim(pair_sum, chip, 1, False)
    for step in range(1, chips):
        target = (chip + step) % chips
        outgoing = lax.dynamic_index_in_dim(pair_sum, target, 1, False).astype(jnp.bfloat16)
        pairs = [(j, (j + 2 * step) % count) for j in range(count)]
        total = total + lax.ppermute(outgoing, axis, pairs).astype(jnp.float32)
    gate = total[:, :, :block_units]
    up = total[:, :, block_units:]
    mine = (jax.nn.silu(gate) * up).astype(jnp.bfloat16)
    gathered = [mine]
    for step in range(1, chips):
        pairs = [(j, (j + 2 * step) % count) for j in range(count)]
        gathered.append(lax.ppermute(mine, axis, pairs))
    stacked = jnp.stack(gathered, axis=1)
    ordered = jnp.take(stacked, (chip - jnp.arange(chips)) % chips, axis=1)
    other = lax.ppermute(ordered, axis, sibling)
    both = jnp.stack([ordered, other], axis=2)
    full = jnp.take(both, jnp.arange(2) ^ core, axis=2)
    return full.reshape(blocks_here, rows, block_units)


def per_device(
    tokens,
    queries,
    key_rows,
    values,
    log_decay,
    head_gain,
    expert_gain,
    route_ids,
    route_weight,
    expert_in,
    expert_out,
):
    length = tokens.shape[0]
    local_width = tokens.shape[1]
    heads_here = log_decay.shape[0]
    head_size = queries.shape[1] // heads_here
    score_scale = head_size ** (-0.5)
    query_heads = queries.reshape(length, heads_here, head_size)
    key_heads = key_rows.reshape(length, heads_here, head_size)
    value_heads = values.reshape(length, heads_here, head_size)
    cumulative = jnp.cumsum(log_decay, axis=1)
    causal = (jnp.arange(length)[:, None] >= jnp.arange(length)[None, :])[None]
    scores = (
        jnp.einsum("thd,shd->hts", query_heads, key_heads, preferred_element_type=jnp.float32)
        * score_scale
    )
    spread = cumulative[:, :, None] - cumulative[:, None, :]
    mixing = jnp.where(causal, scores * jnp.exp(jnp.where(causal, spread, 0.0)), 0.0).astype(
        jnp.bfloat16
    )
    inside = jnp.einsum("hts,shd->thd", mixing, value_heads, preferred_element_type=jnp.float32)
    to_end = jnp.exp(cumulative[:, -1:] - cumulative)
    carried_keys = (key_heads.astype(jnp.float32) * to_end.T[:, :, None]).astype(jnp.bfloat16)
    block_state = jnp.einsum(
        "shd,she->hde", carried_keys, value_heads, preferred_element_type=jnp.float32
    )
    block_decay = jnp.exp(cumulative[:, -1])
    entering = exclusive_scan(block_decay, block_state, "seq")
    from_before = jnp.einsum(
        "thd,hde->the",
        query_heads.astype(jnp.float32),
        entering,
        precision=lax.Precision.HIGHEST,
        preferred_element_type=jnp.float32,
    )
    attended = inside + from_before * (jnp.exp(cumulative).T[:, :, None] * score_scale)
    head_rms = lax.rsqrt(jnp.mean(attended * attended, axis=2, keepdims=True) + EPSILON)
    normed_heads = (attended * head_rms).reshape(length, local_width)
    hidden_state = (tokens.astype(jnp.float32) + normed_heads * head_gain).astype(jnp.bfloat16)
    hidden_wide = hidden_state.astype(jnp.float32)
    local_squares = jnp.sum(hidden_wide * hidden_wide, axis=1)
    total_squares = lax.psum(local_squares, "head")
    inverse_rms = lax.rsqrt(total_squares / D + EPSILON)
    expert_input = (hidden_wide * inverse_rms[:, None] * expert_gain).astype(jnp.bfloat16)
    capacity = CAP
    expert_count = EXPERTS
    flat_ids = route_ids.reshape(-1)
    pair_count = flat_ids.shape[0]
    chosen = (flat_ids[:, None] == jnp.arange(expert_count)[None, :]).astype(jnp.float32)
    strictly_before = (jnp.arange(pair_count)[:, None] > jnp.arange(pair_count)[None, :]).astype(
        jnp.float32
    )
    earlier_counts = jnp.dot(
        strictly_before, chosen, precision=lax.Precision.HIGHEST, preferred_element_type=jnp.float32
    )
    slot_index = jnp.sum(earlier_counts * chosen, axis=1).astype(jnp.int32)
    position = (flat_ids * capacity + slot_index).reshape(length, route_ids.shape[1])
    slot_ids = jnp.arange(expert_count * capacity, dtype=jnp.int32)
    picks = position[None, :, :] == slot_ids[:, None, None]
    dispatch_matrix = jnp.any(picks, axis=2).astype(jnp.bfloat16)
    send_rows = jnp.dot(dispatch_matrix, expert_input, preferred_element_type=jnp.float32).astype(
        jnp.bfloat16
    )
    hidden_split = expert_in.shape[0] * lax.axis_size("seq") // expert_count
    send_buffer = jnp.repeat(
        send_rows.reshape(expert_count, 1, capacity, local_width), hidden_split, axis=0
    )
    block_units = expert_out.shape[1]
    arrived = lax.all_to_all(send_buffer, "seq", split_axis=0, concat_axis=1, tiled=True)
    blocks_here, sources, item_count, feature_count = arrived.shape
    flat_rows = arrived.reshape(blocks_here, sources * item_count, feature_count)
    partial_sums = jnp.einsum(
        "erd,edh->erh", flat_rows, expert_in, preferred_element_type=jnp.float32
    )
    activated = head_reduce_activate(partial_sums.astype(jnp.bfloat16), "head", block_units)
    produced = jnp.einsum(
        "erh,ehd->erd", activated, expert_out, preferred_element_type=jnp.float32
    ).astype(jnp.bfloat16)
    computed = produced.reshape(blocks_here, sources, item_count, feature_count)
    returned = lax.all_to_all(computed, "seq", split_axis=1, concat_axis=0, tiled=True)
    merged = jnp.sum(
        returned.reshape(expert_count, hidden_split, capacity, local_width).astype(jnp.float32),
        axis=1,
    )
    merged = merged.reshape(expert_count * capacity, local_width)
    slot_rows = merged[position]
    expert_mix = jnp.sum(slot_rows * route_weight[:, :, None], axis=1)
    return (hidden_wide + expert_mix).astype(jnp.bfloat16)


def solution(mesh):
    return jax.shard_map(
        per_device,
        mesh=mesh,
        in_specs=(
            P("seq", "head"),
            P("seq", "head"),
            P("seq", "head"),
            P("seq", "head"),
            P("head", "seq"),
            P("head"),
            P("head"),
            P("seq", None),
            P("seq", None),
            P("seq", "head", None),
            P("seq", None, "head"),
        ),
        out_specs=P("seq", "head"),
        check_vma=False,
    )
```

```python
import jax
import jax.numpy as jnp
from jax import lax
from jax.sharding import PartitionSpec as P

D = 4096
EXPERTS = 32
CAP = 20


EPSILON = 1e-06


def pack_window(decay, state):
    heads, rows, cols = state.shape
    high = decay.astype(jnp.bfloat16)
    low = (decay - high.astype(jnp.float32)).astype(jnp.bfloat16)
    tail = jnp.broadcast_to(jnp.stack([high, low], axis=1)[:, :, None], (heads, 2, cols))
    return jnp.concatenate([state.astype(jnp.bfloat16), tail], axis=1)


def exclusive_scan(decay, state, axis):
    place = lax.axis_index(axis)
    count = lax.axis_size(axis)
    rows = state.shape[1]
    window_decay = decay
    window_state = state
    before_decay = jnp.ones_like(decay)
    before_state = jnp.zeros_like(state)
    shift = 1
    while shift < count:
        pairs = [(j, j + shift) for j in range(count - shift)]
        got = lax.ppermute(pack_window(window_decay, window_state), axis, pairs)
        valid = place >= shift
        got_state = got[:, :rows, :].astype(jnp.float32)
        got_decay = got[:, rows, 0].astype(jnp.float32) + got[:, rows + 1, 0].astype(jnp.float32)
        got_decay = jnp.where(valid, got_decay, 1.0)
        before_state = before_decay[:, None, None] * got_state + before_state
        before_decay = before_decay * got_decay
        window_state = window_decay[:, None, None] * got_state + window_state
        window_decay = window_decay * got_decay
        shift *= 2
    return before_state


def head_reduce_activate(partial, axis, block_units):
    place = lax.axis_index(axis)
    count = lax.axis_size(axis)
    chips = count // 2
    core = place % 2
    chip = place // 2
    blocks_here, rows, width = partial.shape
    share = rows // count
    pieces = partial.reshape(blocks_here, chips, 2, share, width)
    sibling = [(j, j ^ 1) for j in range(count)]
    kept = lax.dynamic_index_in_dim(pieces, core, 2, False).astype(jnp.float32)
    handed = lax.dynamic_index_in_dim(pieces, 1 - core, 2, False)
    pair_sum = kept + lax.ppermute(handed, axis, sibling).astype(jnp.float32)
    total = lax.dynamic_index_in_dim(pair_sum, chip, 1, False)
    for step in range(1, chips):
        target = (chip + step) % chips
        outgoing = lax.dynamic_index_in_dim(pair_sum, target, 1, False).astype(jnp.bfloat16)
        pairs = [(j, (j + 2 * step) % count) for j in range(count)]
        total = total + lax.ppermute(outgoing, axis, pairs).astype(jnp.float32)
    gate = total[:, :, :block_units]
    up = total[:, :, block_units:]
    mine = (jax.nn.silu(gate) * up).astype(jnp.bfloat16)
    gathered = [mine]
    for step in range(1, chips):
        pairs = [(j, (j + 2 * step) % count) for j in range(count)]
        gathered.append(lax.ppermute(mine, axis, pairs))
    stacked = jnp.stack(gathered, axis=1)
    ordered = jnp.take(stacked, (chip - jnp.arange(chips)) % chips, axis=1)
    other = lax.ppermute(ordered, axis, sibling)
    both = jnp.stack([ordered, other], axis=2)
    full = jnp.take(both, jnp.arange(2) ^ core, axis=2)
    return full.reshape(blocks_here, rows, block_units)


def per_device(
    tokens,
    queries,
    key_rows,
    values,
    log_decay,
    head_gain,
    expert_gain,
    route_ids,
    route_weight,
    expert_in,
    expert_out,
):
    length = tokens.shape[0]
    local_width = tokens.shape[1]
    heads_here = log_decay.shape[0]
    head_size = queries.shape[1] // heads_here
    score_scale = head_size ** (-0.5)
    query_heads = queries.reshape(length, heads_here, head_size)
    key_heads = key_rows.reshape(length, heads_here, head_size)
    value_heads = values.reshape(length, heads_here, head_size)
    cumulative = jnp.cumsum(log_decay, axis=1)
    causal = (jnp.arange(length)[:, None] >= jnp.arange(length)[None, :])[None]
    scores = (
        jnp.einsum("thd,shd->hts", query_heads, key_heads, preferred_element_type=jnp.float32)
        * score_scale
    )
    spread = cumulative[:, :, None] - cumulative[:, None, :]
    mixing = jnp.where(causal, scores * jnp.exp(jnp.where(causal, spread, 0.0)), 0.0).astype(
        jnp.bfloat16
    )
    inside = jnp.einsum("hts,shd->thd", mixing, value_heads, preferred_element_type=jnp.float32)
    to_end = jnp.exp(cumulative[:, -1:] - cumulative)
    carried_keys = (key_heads.astype(jnp.float32) * to_end.T[:, :, None]).astype(jnp.bfloat16)
    block_state = jnp.einsum(
        "shd,she->hde", carried_keys, value_heads, preferred_element_type=jnp.float32
    )
    block_decay = jnp.exp(cumulative[:, -1])
    entering = exclusive_scan(block_decay, block_state, "seq")
    from_before = jnp.einsum(
        "thd,hde->the",
        query_heads.astype(jnp.float32),
        entering,
        precision=lax.Precision.HIGHEST,
        preferred_element_type=jnp.float32,
    )
    attended = inside + from_before * (jnp.exp(cumulative).T[:, :, None] * score_scale)
    head_rms = lax.rsqrt(jnp.mean(attended * attended, axis=2, keepdims=True) + EPSILON)
    normed_heads = (attended * head_rms).reshape(length, local_width)
    hidden_state = (tokens.astype(jnp.float32) + normed_heads * head_gain).astype(jnp.bfloat16)
    hidden_wide = hidden_state.astype(jnp.float32)
    local_squares = jnp.sum(hidden_wide * hidden_wide, axis=1)
    total_squares = lax.psum(local_squares, "head")
    inverse_rms = lax.rsqrt(total_squares / D + EPSILON)
    expert_input = (hidden_wide * inverse_rms[:, None] * expert_gain).astype(jnp.bfloat16)
    capacity = CAP
    expert_count = EXPERTS
    flat_ids = route_ids.reshape(-1)
    pair_count = flat_ids.shape[0]
    chosen = (flat_ids[:, None] == jnp.arange(expert_count)[None, :]).astype(jnp.float32)
    strictly_before = (jnp.arange(pair_count)[:, None] > jnp.arange(pair_count)[None, :]).astype(
        jnp.float32
    )
    earlier_counts = jnp.dot(
        strictly_before, chosen, precision=lax.Precision.HIGHEST, preferred_element_type=jnp.float32
    )
    slot_index = jnp.sum(earlier_counts * chosen, axis=1).astype(jnp.int32)
    position = (flat_ids * capacity + slot_index).reshape(length, route_ids.shape[1])
    slot_ids = jnp.arange(expert_count * capacity, dtype=jnp.int32)
    picks = position[None, :, :] == slot_ids[:, None, None]
    dispatch_matrix = jnp.any(picks, axis=2).astype(jnp.bfloat16)
    send_rows = jnp.dot(dispatch_matrix, expert_input, preferred_element_type=jnp.float32).astype(
        jnp.bfloat16
    )
    half = capacity // 2
    parity = lax.axis_index("seq") % 2
    partner = [(j, j ^ 1) for j in range(lax.axis_size("seq"))]
    send_buffer = send_rows.reshape(expert_count * 2, 1, half, local_width)
    block_units = expert_out.shape[1]
    arrived = lax.all_to_all(send_buffer, "seq", split_axis=0, concat_axis=1, tiled=True)
    swapped = lax.ppermute(arrived, "seq", partner)
    both = jnp.stack([arrived, swapped], axis=2)
    arrived = jnp.take(both, jnp.arange(2) ^ parity, axis=2)
    blocks_here, sources = arrived.shape[0], arrived.shape[1]
    feature_count = arrived.shape[-1]
    flat_rows = arrived.reshape(blocks_here, sources * capacity, feature_count)
    partial_sums = jnp.einsum(
        "erd,edh->erh", flat_rows, expert_in, preferred_element_type=jnp.float32
    )
    activated = head_reduce_activate(partial_sums.astype(jnp.bfloat16), "head", block_units)
    produced = jnp.einsum(
        "erh,ehd->erd", activated, expert_out, preferred_element_type=jnp.float32
    ).astype(jnp.bfloat16)
    computed = produced.reshape(blocks_here, sources, 2, half, feature_count)
    kept = lax.dynamic_index_in_dim(computed, parity, 2, False).astype(jnp.float32)
    given = lax.dynamic_index_in_dim(computed, 1 - parity, 2, False)
    summed = (kept + lax.ppermute(given, "seq", partner).astype(jnp.float32)).astype(jnp.bfloat16)
    returned = lax.all_to_all(summed, "seq", split_axis=1, concat_axis=0, tiled=True)
    merged = returned.reshape(expert_count, capacity, local_width).astype(jnp.float32)
    merged = merged.reshape(expert_count * capacity, local_width)
    slot_rows = merged[position]
    expert_mix = jnp.sum(slot_rows * route_weight[:, :, None], axis=1)
    return (hidden_wide + expert_mix).astype(jnp.bfloat16)


def solution(mesh):
    return jax.shard_map(
        per_device,
        mesh=mesh,
        in_specs=(
            P("seq", "head"),
            P("seq", "head"),
            P("seq", "head"),
            P("seq", "head"),
            P("head", "seq"),
            P("head"),
            P("head"),
            P("seq", None),
            P("seq", None),
            P("seq", "head", None),
            P("seq", None, "head"),
        ),
        out_specs=P("seq", "head"),
        check_vma=False,
    )
```

```python
import jax
import jax.numpy as jnp
from jax import lax
from jax.sharding import PartitionSpec as P

D = 4096
EXPERTS = 32
CAP = 20
SEQ = ("sx", "sz")
Z_CHIPS = 16


EPSILON = 1e-06


def pack_window(decay, state):
    heads, rows, cols = state.shape
    high = decay.astype(jnp.bfloat16)
    low = (decay - high.astype(jnp.float32)).astype(jnp.bfloat16)
    tail = jnp.broadcast_to(jnp.stack([high, low], axis=1)[:, :, None], (heads, 2, cols))
    return jnp.concatenate([state.astype(jnp.bfloat16), tail], axis=1)


def exclusive_scan(decay, state, axis):
    place = lax.axis_index(axis)
    count = lax.axis_size(axis)
    rows = state.shape[1]
    window_decay = decay
    window_state = state
    before_decay = jnp.ones_like(decay)
    before_state = jnp.zeros_like(state)
    shift = 1
    while shift < count:
        pairs = [(j, j + shift) for j in range(count - shift)]
        got = lax.ppermute(pack_window(window_decay, window_state), axis, pairs)
        valid = place >= shift
        got_state = got[:, :rows, :].astype(jnp.float32)
        got_decay = got[:, rows, 0].astype(jnp.float32) + got[:, rows + 1, 0].astype(jnp.float32)
        got_decay = jnp.where(valid, got_decay, 1.0)
        before_state = before_decay[:, None, None] * got_state + before_state
        before_decay = before_decay * got_decay
        window_state = window_decay[:, None, None] * got_state + window_state
        window_decay = window_decay * got_decay
        shift *= 2
    return before_state


def head_reduce_activate(partial, axis, block_units):
    place = lax.axis_index(axis)
    count = lax.axis_size(axis)
    chips = count // 2
    core = place % 2
    chip = place // 2
    blocks_here, rows, width = partial.shape
    share = rows // count
    pieces = partial.reshape(blocks_here, chips, 2, share, width)
    sibling = [(j, j ^ 1) for j in range(count)]
    kept = lax.dynamic_index_in_dim(pieces, core, 2, False).astype(jnp.float32)
    handed = lax.dynamic_index_in_dim(pieces, 1 - core, 2, False)
    pair_sum = kept + lax.ppermute(handed, axis, sibling).astype(jnp.float32)
    total = lax.dynamic_index_in_dim(pair_sum, chip, 1, False)
    for step in range(1, chips):
        target = (chip + step) % chips
        outgoing = lax.dynamic_index_in_dim(pair_sum, target, 1, False).astype(jnp.bfloat16)
        pairs = [(j, (j + 2 * step) % count) for j in range(count)]
        total = total + lax.ppermute(outgoing, axis, pairs).astype(jnp.float32)
    gate = total[:, :, :block_units]
    up = total[:, :, block_units:]
    mine = (jax.nn.silu(gate) * up).astype(jnp.bfloat16)
    gathered = [mine]
    for step in range(1, chips):
        pairs = [(j, (j + 2 * step) % count) for j in range(count)]
        gathered.append(lax.ppermute(mine, axis, pairs))
    stacked = jnp.stack(gathered, axis=1)
    ordered = jnp.take(stacked, (chip - jnp.arange(chips)) % chips, axis=1)
    other = lax.ppermute(ordered, axis, sibling)
    both = jnp.stack([ordered, other], axis=2)
    full = jnp.take(both, jnp.arange(2) ^ core, axis=2)
    return full.reshape(blocks_here, rows, block_units)


def per_device(
    tokens,
    queries,
    key_rows,
    values,
    log_decay,
    head_gain,
    expert_gain,
    route_ids,
    route_weight,
    expert_in,
    expert_out,
):
    length = tokens.shape[0]
    local_width = tokens.shape[1]
    heads_here = log_decay.shape[0]
    head_size = queries.shape[1] // heads_here
    score_scale = head_size ** (-0.5)
    query_heads = queries.reshape(length, heads_here, head_size)
    key_heads = key_rows.reshape(length, heads_here, head_size)
    value_heads = values.reshape(length, heads_here, head_size)
    cumulative = jnp.cumsum(log_decay, axis=1)
    causal = (jnp.arange(length)[:, None] >= jnp.arange(length)[None, :])[None]
    scores = (
        jnp.einsum("thd,shd->hts", query_heads, key_heads, preferred_element_type=jnp.float32)
        * score_scale
    )
    spread = cumulative[:, :, None] - cumulative[:, None, :]
    mixing = jnp.where(causal, scores * jnp.exp(jnp.where(causal, spread, 0.0)), 0.0).astype(
        jnp.bfloat16
    )
    inside = jnp.einsum("hts,shd->thd", mixing, value_heads, preferred_element_type=jnp.float32)
    to_end = jnp.exp(cumulative[:, -1:] - cumulative)
    carried_keys = (key_heads.astype(jnp.float32) * to_end.T[:, :, None]).astype(jnp.bfloat16)
    block_state = jnp.einsum(
        "shd,she->hde", carried_keys, value_heads, preferred_element_type=jnp.float32
    )
    block_decay = jnp.exp(cumulative[:, -1])
    entering = exclusive_scan(block_decay, block_state, SEQ)
    from_before = jnp.einsum(
        "thd,hde->the",
        query_heads.astype(jnp.float32),
        entering,
        precision=lax.Precision.HIGHEST,
        preferred_element_type=jnp.float32,
    )
    attended = inside + from_before * (jnp.exp(cumulative).T[:, :, None] * score_scale)
    head_rms = lax.rsqrt(jnp.mean(attended * attended, axis=2, keepdims=True) + EPSILON)
    normed_heads = (attended * head_rms).reshape(length, local_width)
    hidden_state = (tokens.astype(jnp.float32) + normed_heads * head_gain).astype(jnp.bfloat16)
    hidden_wide = hidden_state.astype(jnp.float32)
    local_squares = jnp.sum(hidden_wide * hidden_wide, axis=1)
    total_squares = lax.psum(local_squares, "head")
    inverse_rms = lax.rsqrt(total_squares / D + EPSILON)
    expert_input = (hidden_wide * inverse_rms[:, None] * expert_gain).astype(jnp.bfloat16)
    capacity = CAP
    expert_count = EXPERTS
    flat_ids = route_ids.reshape(-1)
    pair_count = flat_ids.shape[0]
    chosen = (flat_ids[:, None] == jnp.arange(expert_count)[None, :]).astype(jnp.float32)
    strictly_before = (jnp.arange(pair_count)[:, None] > jnp.arange(pair_count)[None, :]).astype(
        jnp.float32
    )
    earlier_counts = jnp.dot(
        strictly_before, chosen, precision=lax.Precision.HIGHEST, preferred_element_type=jnp.float32
    )
    slot_index = jnp.sum(earlier_counts * chosen, axis=1).astype(jnp.int32)
    position = (flat_ids * capacity + slot_index).reshape(length, route_ids.shape[1])
    slot_ids = jnp.arange(expert_count * capacity, dtype=jnp.int32)
    picks = position[None, :, :] == slot_ids[:, None, None]
    dispatch_matrix = jnp.any(picks, axis=2).astype(jnp.bfloat16)
    send_rows = jnp.dot(dispatch_matrix, expert_input, preferred_element_type=jnp.float32).astype(
        jnp.bfloat16
    )
    hidden_split = expert_in.shape[0] * lax.axis_size(SEQ) // expert_count
    send_buffer = jnp.repeat(
        send_rows.reshape(expert_count, 1, capacity, local_width), hidden_split, axis=0
    )
    block_units = expert_out.shape[1]
    rows_x = lax.axis_size("sx")
    rows_z = lax.axis_size("sz")
    staged = send_buffer.reshape(rows_x, rows_z, capacity, local_width)
    staged = lax.all_to_all(staged, "sz", split_axis=1, concat_axis=1, tiled=True)
    staged = lax.all_to_all(staged, "sx", split_axis=0, concat_axis=0, tiled=True)
    arrived = staged.reshape(1, rows_x * rows_z, capacity, local_width)
    blocks_here, sources, item_count, feature_count = arrived.shape
    flat_rows = arrived.reshape(blocks_here, sources * item_count, feature_count)
    partial_sums = jnp.einsum(
        "erd,edh->erh", flat_rows, expert_in, preferred_element_type=jnp.float32
    )
    activated = head_reduce_activate(partial_sums.astype(jnp.bfloat16), "head", block_units)
    produced = jnp.einsum(
        "erh,ehd->erd", activated, expert_out, preferred_element_type=jnp.float32
    ).astype(jnp.bfloat16)
    computed = produced.reshape(blocks_here, sources, item_count, feature_count)
    staged = computed.reshape(rows_x, rows_z, capacity, local_width)
    staged = lax.all_to_all(staged, "sx", split_axis=0, concat_axis=0, tiled=True)
    staged = lax.all_to_all(staged, "sz", split_axis=1, concat_axis=1, tiled=True)
    returned = staged.reshape(rows_x * rows_z, 1, capacity, local_width)
    merged = jnp.sum(
        returned.reshape(expert_count, hidden_split, capacity, local_width).astype(jnp.float32),
        axis=1,
    )
    merged = merged.reshape(expert_count * capacity, local_width)
    slot_rows = merged[position]
    expert_mix = jnp.sum(slot_rows * route_weight[:, :, None], axis=1)
    return (hidden_wide + expert_mix).astype(jnp.bfloat16)


def solution(mesh):
    seq_count = mesh.shape["seq"]
    split = mesh.devices.reshape(seq_count // Z_CHIPS, Z_CHIPS, mesh.shape["head"])
    mesh = jax.sharding.Mesh(split, ("sx", "sz", "head"))
    return jax.shard_map(
        per_device,
        mesh=mesh,
        in_specs=(
            P(SEQ, "head"),
            P(SEQ, "head"),
            P(SEQ, "head"),
            P(SEQ, "head"),
            P("head", SEQ),
            P("head"),
            P("head"),
            P(SEQ, None),
            P(SEQ, None),
            P(SEQ, "head", None),
            P(SEQ, None, "head"),
        ),
        out_specs=P(SEQ, "head"),
        check_vma=False,
    )
```

```python
import jax
import jax.numpy as jnp
from jax import lax
from jax.sharding import PartitionSpec as P

D = 4096
EXPERTS = 32
CAP = 20


EPSILON = 1e-06


def pack_window(decay, state):
    heads, rows, cols = state.shape
    high = decay.astype(jnp.bfloat16)
    low = (decay - high.astype(jnp.float32)).astype(jnp.bfloat16)
    tail = jnp.broadcast_to(jnp.stack([high, low], axis=1)[:, :, None], (heads, 2, cols))
    return jnp.concatenate([state.astype(jnp.bfloat16), tail], axis=1)


def unpack_window(got, rows):
    got_state = got[:, :rows, :].astype(jnp.float32)
    got_decay = got[:, rows, 0].astype(jnp.float32) + got[:, rows + 1, 0].astype(jnp.float32)
    return got_decay, got_state


def exclusive_scan(decay, state, axis):
    place = lax.axis_index(axis)
    count = lax.axis_size(axis)
    rows = state.shape[1]
    cur_decay = decay
    cur_state = state
    span = 1
    while span < count:
        ends = [i for i in range(count) if (i + 1) % (2 * span) == 0]
        got = lax.ppermute(
            pack_window(cur_decay, cur_state), axis, [(i - span, i) for i in ends]
        )
        got_decay, got_state = unpack_window(got, rows)
        take = (place + 1) % (2 * span) == 0
        cur_state = jnp.where(take, cur_decay[:, None, None] * got_state + cur_state, cur_state)
        cur_decay = jnp.where(take, cur_decay * got_decay, cur_decay)
        span *= 2
    last = place == count - 1
    cur_state = jnp.where(last, 0.0, cur_state)
    cur_decay = jnp.where(last, 1.0, cur_decay)
    span = count // 2
    while span >= 1:
        ends = [i for i in range(count) if (i + 1) % (2 * span) == 0]
        packed = pack_window(cur_decay, cur_state)
        leftward = lax.ppermute(packed, axis, [(i, i - span) for i in ends])
        rightward = lax.ppermute(packed, axis, [(i - span, i) for i in ends])
        prefix_decay, prefix_state = unpack_window(leftward, rows)
        total_decay, total_state = unpack_window(rightward, rows)
        is_right = (place + 1) % (2 * span) == 0
        is_left = (place + 1) % (2 * span) == span
        right_state = total_decay[:, None, None] * cur_state + total_state
        right_decay = cur_decay * total_decay
        cur_state = jnp.where(is_right, right_state, jnp.where(is_left, prefix_state, cur_state))
        cur_decay = jnp.where(is_right, right_decay, jnp.where(is_left, prefix_decay, cur_decay))
        span //= 2
    return cur_state


def head_reduce_activate(partial, axis, block_units):
    place = lax.axis_index(axis)
    count = lax.axis_size(axis)
    chips = count // 2
    core = place % 2
    chip = place // 2
    blocks_here, rows, width = partial.shape
    share = rows // count
    pieces = partial.reshape(blocks_here, chips, 2, share, width)
    sibling = [(j, j ^ 1) for j in range(count)]
    kept = lax.dynamic_index_in_dim(pieces, core, 2, False).astype(jnp.float32)
    handed = lax.dynamic_index_in_dim(pieces, 1 - core, 2, False)
    pair_sum = kept + lax.ppermute(handed, axis, sibling).astype(jnp.float32)
    total = lax.dynamic_index_in_dim(pair_sum, chip, 1, False)
    for step in range(1, chips):
        target = (chip + step) % chips
        outgoing = lax.dynamic_index_in_dim(pair_sum, target, 1, False).astype(jnp.bfloat16)
        pairs = [(j, (j + 2 * step) % count) for j in range(count)]
        total = total + lax.ppermute(outgoing, axis, pairs).astype(jnp.float32)
    gate = total[:, :, :block_units]
    up = total[:, :, block_units:]
    mine = (jax.nn.silu(gate) * up).astype(jnp.bfloat16)
    gathered = [mine]
    for step in range(1, chips):
        pairs = [(j, (j + 2 * step) % count) for j in range(count)]
        gathered.append(lax.ppermute(mine, axis, pairs))
    stacked = jnp.stack(gathered, axis=1)
    ordered = jnp.take(stacked, (chip - jnp.arange(chips)) % chips, axis=1)
    other = lax.ppermute(ordered, axis, sibling)
    both = jnp.stack([ordered, other], axis=2)
    full = jnp.take(both, jnp.arange(2) ^ core, axis=2)
    return full.reshape(blocks_here, rows, block_units)


def per_device(
    tokens,
    queries,
    key_rows,
    values,
    log_decay,
    head_gain,
    expert_gain,
    route_ids,
    route_weight,
    expert_in,
    expert_out,
):
    length = tokens.shape[0]
    local_width = tokens.shape[1]
    heads_here = log_decay.shape[0]
    head_size = queries.shape[1] // heads_here
    score_scale = head_size ** (-0.5)
    query_heads = queries.reshape(length, heads_here, head_size)
    key_heads = key_rows.reshape(length, heads_here, head_size)
    value_heads = values.reshape(length, heads_here, head_size)
    cumulative = jnp.cumsum(log_decay, axis=1)
    causal = (jnp.arange(length)[:, None] >= jnp.arange(length)[None, :])[None]
    scores = (
        jnp.einsum("thd,shd->hts", query_heads, key_heads, preferred_element_type=jnp.float32)
        * score_scale
    )
    spread = cumulative[:, :, None] - cumulative[:, None, :]
    mixing = jnp.where(causal, scores * jnp.exp(jnp.where(causal, spread, 0.0)), 0.0).astype(
        jnp.bfloat16
    )
    inside = jnp.einsum("hts,shd->thd", mixing, value_heads, preferred_element_type=jnp.float32)
    to_end = jnp.exp(cumulative[:, -1:] - cumulative)
    carried_keys = (key_heads.astype(jnp.float32) * to_end.T[:, :, None]).astype(jnp.bfloat16)
    block_state = jnp.einsum(
        "shd,she->hde", carried_keys, value_heads, preferred_element_type=jnp.float32
    )
    block_decay = jnp.exp(cumulative[:, -1])
    entering = exclusive_scan(block_decay, block_state, "seq")
    from_before = jnp.einsum(
        "thd,hde->the",
        query_heads.astype(jnp.float32),
        entering,
        precision=lax.Precision.HIGHEST,
        preferred_element_type=jnp.float32,
    )
    attended = inside + from_before * (jnp.exp(cumulative).T[:, :, None] * score_scale)
    head_rms = lax.rsqrt(jnp.mean(attended * attended, axis=2, keepdims=True) + EPSILON)
    normed_heads = (attended * head_rms).reshape(length, local_width)
    hidden_state = (tokens.astype(jnp.float32) + normed_heads * head_gain).astype(jnp.bfloat16)
    hidden_wide = hidden_state.astype(jnp.float32)
    local_squares = jnp.sum(hidden_wide * hidden_wide, axis=1)
    total_squares = lax.psum(local_squares, "head")
    inverse_rms = lax.rsqrt(total_squares / D + EPSILON)
    expert_input = (hidden_wide * inverse_rms[:, None] * expert_gain).astype(jnp.bfloat16)
    capacity = CAP
    expert_count = EXPERTS
    flat_ids = route_ids.reshape(-1)
    pair_count = flat_ids.shape[0]
    chosen = (flat_ids[:, None] == jnp.arange(expert_count)[None, :]).astype(jnp.float32)
    strictly_before = (jnp.arange(pair_count)[:, None] > jnp.arange(pair_count)[None, :]).astype(
        jnp.float32
    )
    earlier_counts = jnp.dot(
        strictly_before, chosen, precision=lax.Precision.HIGHEST, preferred_element_type=jnp.float32
    )
    slot_index = jnp.sum(earlier_counts * chosen, axis=1).astype(jnp.int32)
    position = (flat_ids * capacity + slot_index).reshape(length, route_ids.shape[1])
    slot_ids = jnp.arange(expert_count * capacity, dtype=jnp.int32)
    picks = position[None, :, :] == slot_ids[:, None, None]
    dispatch_matrix = jnp.any(picks, axis=2).astype(jnp.bfloat16)
    send_rows = jnp.dot(dispatch_matrix, expert_input, preferred_element_type=jnp.float32).astype(
        jnp.bfloat16
    )
    hidden_split = expert_in.shape[0] * lax.axis_size("seq") // expert_count
    send_buffer = jnp.repeat(
        send_rows.reshape(expert_count, 1, capacity, local_width), hidden_split, axis=0
    )
    block_units = expert_out.shape[1]
    arrived = lax.all_to_all(send_buffer, "seq", split_axis=0, concat_axis=1, tiled=True)
    blocks_here, sources, item_count, feature_count = arrived.shape
    flat_rows = arrived.reshape(blocks_here, sources * item_count, feature_count)
    partial_sums = jnp.einsum(
        "erd,edh->erh", flat_rows, expert_in, preferred_element_type=jnp.float32
    )
    activated = head_reduce_activate(partial_sums.astype(jnp.bfloat16), "head", block_units)
    produced = jnp.einsum(
        "erh,ehd->erd", activated, expert_out, preferred_element_type=jnp.float32
    ).astype(jnp.bfloat16)
    computed = produced.reshape(blocks_here, sources, item_count, feature_count)
    returned = lax.all_to_all(computed, "seq", split_axis=1, concat_axis=0, tiled=True)
    merged = jnp.sum(
        returned.reshape(expert_count, hidden_split, capacity, local_width).astype(jnp.float32),
        axis=1,
    )
    merged = merged.reshape(expert_count * capacity, local_width)
    slot_rows = merged[position]
    expert_mix = jnp.sum(slot_rows * route_weight[:, :, None], axis=1)
    return (hidden_wide + expert_mix).astype(jnp.bfloat16)


def solution(mesh):
    return jax.shard_map(
        per_device,
        mesh=mesh,
        in_specs=(
            P("seq", "head"),
            P("seq", "head"),
            P("seq", "head"),
            P("seq", "head"),
            P("head", "seq"),
            P("head"),
            P("head"),
            P("seq", None),
            P("seq", None),
            P("seq", "head", None),
            P("seq", None, "head"),
        ),
        out_specs=P("seq", "head"),
        check_vma=False,
    )
```

```python
import jax
import jax.numpy as jnp
from jax import lax
from jax.sharding import PartitionSpec as P

D = 4096
EXPERTS = 32
CAP = 20


EPSILON = 1e-06


def pack_window(decay, state):
    heads, rows, cols = state.shape
    high = decay.astype(jnp.bfloat16)
    low = (decay - high.astype(jnp.float32)).astype(jnp.bfloat16)
    tail = jnp.broadcast_to(jnp.stack([high, low], axis=1)[:, :, None], (heads, 2, cols))
    return jnp.concatenate([state.astype(jnp.bfloat16), tail], axis=1)


def exclusive_scan(decay, state, axis):
    place = lax.axis_index(axis)
    count = lax.axis_size(axis)
    rows = state.shape[1]
    window_decay = decay
    window_state = state
    before_decay = jnp.ones_like(decay)
    before_state = jnp.zeros_like(state)
    shift = 1
    while shift < count:
        pairs = [(j, j + shift) for j in range(count - shift)]
        got = lax.ppermute(pack_window(window_decay, window_state), axis, pairs)
        valid = place >= shift
        got_state = got[:, :rows, :].astype(jnp.float32)
        got_decay = got[:, rows, 0].astype(jnp.float32) + got[:, rows + 1, 0].astype(jnp.float32)
        got_decay = jnp.where(valid, got_decay, 1.0)
        before_state = before_decay[:, None, None] * got_state + before_state
        before_decay = before_decay * got_decay
        window_state = window_decay[:, None, None] * got_state + window_state
        window_decay = window_decay * got_decay
        shift *= 2
    return before_state


def head_reduce_activate(partial, axis, block_units):
    place = lax.axis_index(axis)
    count = lax.axis_size(axis)
    chips = count // 2
    core = place % 2
    chip = place // 2
    blocks_here, rows, width = partial.shape
    share = rows // count
    pieces = partial.reshape(blocks_here, chips, 2, share, width)
    sibling = [(j, j ^ 1) for j in range(count)]
    kept = lax.dynamic_index_in_dim(pieces, core, 2, False).astype(jnp.float32)
    handed = lax.dynamic_index_in_dim(pieces, 1 - core, 2, False)
    pair_sum = kept + lax.ppermute(handed, axis, sibling).astype(jnp.float32)
    total = lax.dynamic_index_in_dim(pair_sum, chip, 1, False)
    for step in range(1, chips):
        target = (chip + step) % chips
        outgoing = lax.dynamic_index_in_dim(pair_sum, target, 1, False).astype(jnp.bfloat16)
        pairs = [(j, (j + 2 * step) % count) for j in range(count)]
        total = total + lax.ppermute(outgoing, axis, pairs).astype(jnp.float32)
    gate = total[:, :, :block_units]
    up = total[:, :, block_units:]
    mine = (jax.nn.silu(gate) * up).astype(jnp.bfloat16)
    gathered = [mine]
    for step in range(1, chips):
        pairs = [(j, (j + 2 * step) % count) for j in range(count)]
        gathered.append(lax.ppermute(mine, axis, pairs))
    stacked = jnp.stack(gathered, axis=1)
    ordered = jnp.take(stacked, (chip - jnp.arange(chips)) % chips, axis=1)
    other = lax.ppermute(ordered, axis, sibling)
    both = jnp.stack([ordered, other], axis=2)
    full = jnp.take(both, jnp.arange(2) ^ core, axis=2)
    return full.reshape(blocks_here, rows, block_units)


def head_sum(value, axis):
    count = lax.axis_size(axis)
    pair = value + lax.ppermute(value, axis, [(j, j ^ 1) for j in range(count)])
    total = pair
    for step in range(1, count // 2):
        pairs = [(j, (j + 2 * step) % count) for j in range(count)]
        total = total + lax.ppermute(pair, axis, pairs)
    return total


def per_device(
    tokens,
    queries,
    key_rows,
    values,
    log_decay,
    head_gain,
    expert_gain,
    route_ids,
    route_weight,
    expert_in,
    expert_out,
):
    length = tokens.shape[0]
    local_width = tokens.shape[1]
    heads_here = log_decay.shape[0]
    head_size = queries.shape[1] // heads_here
    score_scale = head_size ** (-0.5)
    query_heads = queries.reshape(length, heads_here, head_size)
    key_heads = key_rows.reshape(length, heads_here, head_size)
    value_heads = values.reshape(length, heads_here, head_size)
    cumulative = jnp.cumsum(log_decay, axis=1)
    causal = (jnp.arange(length)[:, None] >= jnp.arange(length)[None, :])[None]
    scores = (
        jnp.einsum("thd,shd->hts", query_heads, key_heads, preferred_element_type=jnp.float32)
        * score_scale
    )
    spread = cumulative[:, :, None] - cumulative[:, None, :]
    mixing = jnp.where(causal, scores * jnp.exp(jnp.where(causal, spread, 0.0)), 0.0).astype(
        jnp.bfloat16
    )
    inside = jnp.einsum("hts,shd->thd", mixing, value_heads, preferred_element_type=jnp.float32)
    to_end = jnp.exp(cumulative[:, -1:] - cumulative)
    carried_keys = (key_heads.astype(jnp.float32) * to_end.T[:, :, None]).astype(jnp.bfloat16)
    block_state = jnp.einsum(
        "shd,she->hde", carried_keys, value_heads, preferred_element_type=jnp.float32
    )
    block_decay = jnp.exp(cumulative[:, -1])
    entering = exclusive_scan(block_decay, block_state, "seq")
    from_before = jnp.einsum(
        "thd,hde->the",
        query_heads.astype(jnp.float32),
        entering,
        precision=lax.Precision.HIGHEST,
        preferred_element_type=jnp.float32,
    )
    attended = inside + from_before * (jnp.exp(cumulative).T[:, :, None] * score_scale)
    head_rms = lax.rsqrt(jnp.mean(attended * attended, axis=2, keepdims=True) + EPSILON)
    normed_heads = (attended * head_rms).reshape(length, local_width)
    hidden_state = (tokens.astype(jnp.float32) + normed_heads * head_gain).astype(jnp.bfloat16)
    hidden_wide = hidden_state.astype(jnp.float32)
    local_squares = jnp.sum(hidden_wide * hidden_wide, axis=1)
    total_squares = head_sum(local_squares, "head")
    inverse_rms = lax.rsqrt(total_squares / D + EPSILON)
    expert_input = (hidden_wide * inverse_rms[:, None] * expert_gain).astype(jnp.bfloat16)
    capacity = CAP
    expert_count = EXPERTS
    flat_ids = route_ids.reshape(-1)
    pair_count = flat_ids.shape[0]
    chosen = (flat_ids[:, None] == jnp.arange(expert_count)[None, :]).astype(jnp.float32)
    strictly_before = (jnp.arange(pair_count)[:, None] > jnp.arange(pair_count)[None, :]).astype(
        jnp.float32
    )
    earlier_counts = jnp.dot(
        strictly_before, chosen, precision=lax.Precision.HIGHEST, preferred_element_type=jnp.float32
    )
    slot_index = jnp.sum(earlier_counts * chosen, axis=1).astype(jnp.int32)
    position = (flat_ids * capacity + slot_index).reshape(length, route_ids.shape[1])
    slot_ids = jnp.arange(expert_count * capacity, dtype=jnp.int32)
    picks = position[None, :, :] == slot_ids[:, None, None]
    dispatch_matrix = jnp.any(picks, axis=2).astype(jnp.bfloat16)
    send_rows = jnp.dot(dispatch_matrix, expert_input, preferred_element_type=jnp.float32).astype(
        jnp.bfloat16
    )
    hidden_split = expert_in.shape[0] * lax.axis_size("seq") // expert_count
    send_buffer = jnp.repeat(
        send_rows.reshape(expert_count, 1, capacity, local_width), hidden_split, axis=0
    )
    block_units = expert_out.shape[1]
    arrived = lax.all_to_all(send_buffer, "seq", split_axis=0, concat_axis=1, tiled=True)
    blocks_here, sources, item_count, feature_count = arrived.shape
    flat_rows = arrived.reshape(blocks_here, sources * item_count, feature_count)
    partial_sums = jnp.einsum(
        "erd,edh->erh", flat_rows, expert_in, preferred_element_type=jnp.float32
    )
    activated = head_reduce_activate(partial_sums.astype(jnp.bfloat16), "head", block_units)
    produced = jnp.einsum(
        "erh,ehd->erd", activated, expert_out, preferred_element_type=jnp.float32
    ).astype(jnp.bfloat16)
    computed = produced.reshape(blocks_here, sources, item_count, feature_count)
    returned = lax.all_to_all(computed, "seq", split_axis=1, concat_axis=0, tiled=True)
    merged = jnp.sum(
        returned.reshape(expert_count, hidden_split, capacity, local_width).astype(jnp.float32),
        axis=1,
    )
    merged = merged.reshape(expert_count * capacity, local_width)
    slot_rows = merged[position]
    expert_mix = jnp.sum(slot_rows * route_weight[:, :, None], axis=1)
    return (hidden_wide + expert_mix).astype(jnp.bfloat16)


def solution(mesh):
    return jax.shard_map(
        per_device,
        mesh=mesh,
        in_specs=(
            P("seq", "head"),
            P("seq", "head"),
            P("seq", "head"),
            P("seq", "head"),
            P("head", "seq"),
            P("head"),
            P("head"),
            P("seq", None),
            P("seq", None),
            P("seq", "head", None),
            P("seq", None, "head"),
        ),
        out_specs=P("seq", "head"),
        check_vma=False,
    )
```

```python
import jax
import jax.numpy as jnp
from jax import lax
from jax.sharding import PartitionSpec as P

D = 4096
EXPERTS = 32
CAP = 20


EPSILON = 1e-06


def pack_window(decay, state):
    heads, rows, cols = state.shape
    high = decay.astype(jnp.bfloat16)
    low = (decay - high.astype(jnp.float32)).astype(jnp.bfloat16)
    tail = jnp.broadcast_to(jnp.stack([high, low], axis=1)[:, :, None], (heads, 2, cols))
    return jnp.concatenate([state.astype(jnp.bfloat16), tail], axis=1)


def exclusive_scan(decay, state, axis):
    place = lax.axis_index(axis)
    count = lax.axis_size(axis)
    rows = state.shape[1]
    window_decay = decay
    window_state = state
    before_decay = jnp.ones_like(decay)
    before_state = jnp.zeros_like(state)
    shift = 1
    while shift < count:
        pairs = [(j, j + shift) for j in range(count - shift)]
        got = lax.ppermute(pack_window(window_decay, window_state), axis, pairs)
        valid = place >= shift
        got_state = got[:, :rows, :].astype(jnp.float32)
        got_decay = got[:, rows, 0].astype(jnp.float32) + got[:, rows + 1, 0].astype(jnp.float32)
        got_decay = jnp.where(valid, got_decay, 1.0)
        before_state = before_decay[:, None, None] * got_state + before_state
        before_decay = before_decay * got_decay
        window_state = window_decay[:, None, None] * got_state + window_state
        window_decay = window_decay * got_decay
        shift *= 2
    return before_state


def head_reduce_activate(partial, axis, block_units):
    place = lax.axis_index(axis)
    count = lax.axis_size(axis)
    chips = count // 2
    core = place % 2
    chip = place // 2
    blocks_here, rows, width = partial.shape
    share = rows // count
    pieces = partial.reshape(blocks_here, chips, 2, share, width)
    sibling = [(j, j ^ 1) for j in range(count)]
    kept = lax.dynamic_index_in_dim(pieces, core, 2, False).astype(jnp.float32)
    handed = lax.dynamic_index_in_dim(pieces, 1 - core, 2, False)
    pair_sum = kept + lax.ppermute(handed, axis, sibling).astype(jnp.float32)
    total = lax.dynamic_index_in_dim(pair_sum, chip, 1, False)
    for step in range(1, chips):
        target = (chip + step) % chips
        outgoing = lax.dynamic_index_in_dim(pair_sum, target, 1, False).astype(jnp.bfloat16)
        pairs = [(j, (j + 2 * step) % count) for j in range(count)]
        total = total + lax.ppermute(outgoing, axis, pairs).astype(jnp.float32)
    split = total.reshape(blocks_here, share, width // (2 * block_units), 2, block_units)
    mine = (jax.nn.silu(split[:, :, :, 0]) * split[:, :, :, 1]).astype(jnp.bfloat16)
    mine = mine.reshape(blocks_here, share, width // 2)
    gathered = [mine]
    for step in range(1, chips):
        pairs = [(j, (j + 2 * step) % count) for j in range(count)]
        gathered.append(lax.ppermute(mine, axis, pairs))
    stacked = jnp.stack(gathered, axis=1)
    ordered = jnp.take(stacked, (chip - jnp.arange(chips)) % chips, axis=1)
    other = lax.ppermute(ordered, axis, sibling)
    both = jnp.stack([ordered, other], axis=2)
    full = jnp.take(both, jnp.arange(2) ^ core, axis=2)
    return full.reshape(blocks_here, rows, width // 2)


def per_device(
    tokens,
    queries,
    key_rows,
    values,
    log_decay,
    head_gain,
    expert_gain,
    route_ids,
    route_weight,
    expert_in,
    expert_out,
):
    parity = lax.axis_index("seq") % 2
    partner = [(j, j ^ 1) for j in range(lax.axis_size("seq"))]
    other_in, other_out = lax.ppermute((expert_in, expert_out), "seq", partner)
    length = tokens.shape[0]
    local_width = tokens.shape[1]
    heads_here = log_decay.shape[0]
    head_size = queries.shape[1] // heads_here
    score_scale = head_size ** (-0.5)
    query_heads = queries.reshape(length, heads_here, head_size)
    key_heads = key_rows.reshape(length, heads_here, head_size)
    value_heads = values.reshape(length, heads_here, head_size)
    cumulative = jnp.cumsum(log_decay, axis=1)
    causal = (jnp.arange(length)[:, None] >= jnp.arange(length)[None, :])[None]
    scores = (
        jnp.einsum("thd,shd->hts", query_heads, key_heads, preferred_element_type=jnp.float32)
        * score_scale
    )
    spread = cumulative[:, :, None] - cumulative[:, None, :]
    mixing = jnp.where(causal, scores * jnp.exp(jnp.where(causal, spread, 0.0)), 0.0).astype(
        jnp.bfloat16
    )
    inside = jnp.einsum("hts,shd->thd", mixing, value_heads, preferred_element_type=jnp.float32)
    to_end = jnp.exp(cumulative[:, -1:] - cumulative)
    carried_keys = (key_heads.astype(jnp.float32) * to_end.T[:, :, None]).astype(jnp.bfloat16)
    block_state = jnp.einsum(
        "shd,she->hde", carried_keys, value_heads, preferred_element_type=jnp.float32
    )
    block_decay = jnp.exp(cumulative[:, -1])
    entering = exclusive_scan(block_decay, block_state, "seq")
    entering, other_in, other_out = lax.optimization_barrier((entering, other_in, other_out))
    from_before = jnp.einsum(
        "thd,hde->the",
        query_heads.astype(jnp.float32),
        entering,
        precision=lax.Precision.HIGHEST,
        preferred_element_type=jnp.float32,
    )
    attended = inside + from_before * (jnp.exp(cumulative).T[:, :, None] * score_scale)
    head_rms = lax.rsqrt(jnp.mean(attended * attended, axis=2, keepdims=True) + EPSILON)
    normed_heads = (attended * head_rms).reshape(length, local_width)
    hidden_state = (tokens.astype(jnp.float32) + normed_heads * head_gain).astype(jnp.bfloat16)
    hidden_wide = hidden_state.astype(jnp.float32)
    local_squares = jnp.sum(hidden_wide * hidden_wide, axis=1)
    total_squares = lax.psum(local_squares, "head")
    inverse_rms = lax.rsqrt(total_squares / D + EPSILON)
    expert_input = (hidden_wide * inverse_rms[:, None] * expert_gain).astype(jnp.bfloat16)
    capacity = CAP
    expert_count = EXPERTS
    flat_ids = route_ids.reshape(-1)
    pair_count = flat_ids.shape[0]
    chosen = (flat_ids[:, None] == jnp.arange(expert_count)[None, :]).astype(jnp.float32)
    strictly_before = (jnp.arange(pair_count)[:, None] > jnp.arange(pair_count)[None, :]).astype(
        jnp.float32
    )
    earlier_counts = jnp.dot(
        strictly_before, chosen, precision=lax.Precision.HIGHEST, preferred_element_type=jnp.float32
    )
    slot_index = jnp.sum(earlier_counts * chosen, axis=1).astype(jnp.int32)
    position = (flat_ids * capacity + slot_index).reshape(length, route_ids.shape[1])
    slot_ids = jnp.arange(expert_count * capacity, dtype=jnp.int32)
    picks = position[None, :, :] == slot_ids[:, None, None]
    dispatch_matrix = jnp.any(picks, axis=2).astype(jnp.bfloat16)
    send_rows = jnp.dot(dispatch_matrix, expert_input, preferred_element_type=jnp.float32).astype(
        jnp.bfloat16
    )
    even = parity == 0
    first_in = jnp.where(even, expert_in, other_in)
    second_in = jnp.where(even, other_in, expert_in)
    first_out = jnp.where(even, expert_out, other_out)
    second_out = jnp.where(even, other_out, expert_out)
    half = capacity // 2
    block_units = expert_out.shape[1]
    send_buffer = send_rows.reshape(expert_count * 2, 1, half, local_width)
    arrived = lax.all_to_all(send_buffer, "seq", split_axis=0, concat_axis=1, tiled=True)
    blocks_here, sources = arrived.shape[0], arrived.shape[1]
    flat_rows = arrived.reshape(blocks_here, sources * half, local_width)
    weight_in = jnp.concatenate([first_in, second_in], axis=2)
    partial_sums = jnp.einsum(
        "erd,edh->erh", flat_rows, weight_in, preferred_element_type=jnp.float32
    )
    activated = head_reduce_activate(partial_sums.astype(jnp.bfloat16), "head", block_units)
    activated = activated.reshape(blocks_here, sources * half, 2, block_units)
    first_part = jnp.einsum(
        "erh,ehd->erd", activated[:, :, 0], first_out, preferred_element_type=jnp.float32
    ).astype(jnp.bfloat16)
    second_part = jnp.einsum(
        "erh,ehd->erd", activated[:, :, 1], second_out, preferred_element_type=jnp.float32
    ).astype(jnp.bfloat16)
    summed = (first_part.astype(jnp.float32) + second_part.astype(jnp.float32)).astype(
        jnp.bfloat16
    )
    summed = summed.reshape(blocks_here, sources, half, local_width)
    returned = lax.all_to_all(summed, "seq", split_axis=1, concat_axis=0, tiled=True)
    merged = returned.reshape(expert_count, capacity, local_width).astype(jnp.float32)
    merged = merged.reshape(expert_count * capacity, local_width)
    slot_rows = merged[position]
    expert_mix = jnp.sum(slot_rows * route_weight[:, :, None], axis=1)
    return (hidden_wide + expert_mix).astype(jnp.bfloat16)


def solution(mesh):
    return jax.shard_map(
        per_device,
        mesh=mesh,
        in_specs=(
            P("seq", "head"),
            P("seq", "head"),
            P("seq", "head"),
            P("seq", "head"),
            P("head", "seq"),
            P("head"),
            P("head"),
            P("seq", None),
            P("seq", None),
            P("seq", "head", None),
            P("seq", None, "head"),
        ),
        out_specs=P("seq", "head"),
        check_vma=False,
    )
```

```python
import jax
import jax.numpy as jnp
from jax import lax
from jax.sharding import PartitionSpec as P

D = 4096
EXPERTS = 32
CAP = 20


EPSILON = 1e-06


def pack_window(decay, state):
    heads, rows, cols = state.shape
    high = decay.astype(jnp.bfloat16)
    low = (decay - high.astype(jnp.float32)).astype(jnp.bfloat16)
    tail = jnp.broadcast_to(jnp.stack([high, low], axis=1)[:, :, None], (heads, 2, cols))
    return jnp.concatenate([state.astype(jnp.bfloat16), tail], axis=1)


def exclusive_scan(decay, state, axis):
    place = lax.axis_index(axis)
    count = lax.axis_size(axis)
    rows = state.shape[1]
    window_decay = decay
    window_state = state
    before_decay = jnp.ones_like(decay)
    before_state = jnp.zeros_like(state)
    shift = 1
    while shift < count:
        pairs = [(j, j + shift) for j in range(count - shift)]
        got = lax.ppermute(pack_window(window_decay, window_state), axis, pairs)
        valid = place >= shift
        got_state = got[:, :rows, :].astype(jnp.float32)
        got_decay = got[:, rows, 0].astype(jnp.float32) + got[:, rows + 1, 0].astype(jnp.float32)
        got_decay = jnp.where(valid, got_decay, 1.0)
        before_state = before_decay[:, None, None] * got_state + before_state
        before_decay = before_decay * got_decay
        window_state = window_decay[:, None, None] * got_state + window_state
        window_decay = window_decay * got_decay
        shift *= 2
    return before_state


def head_reduce_activate(partial, axis, block_units):
    place = lax.axis_index(axis)
    count = lax.axis_size(axis)
    chips = count // 2
    core = place % 2
    chip = place // 2
    blocks_here, rows, width = partial.shape
    share = rows // count
    pieces = partial.reshape(blocks_here, chips, 2, share, width)
    sibling = [(j, j ^ 1) for j in range(count)]
    kept = lax.dynamic_index_in_dim(pieces, core, 2, False).astype(jnp.float32)
    handed = lax.dynamic_index_in_dim(pieces, 1 - core, 2, False)
    pair_sum = kept + lax.ppermute(handed, axis, sibling).astype(jnp.float32)
    total = lax.dynamic_index_in_dim(pair_sum, chip, 1, False)
    for step in range(1, chips):
        target = (chip + step) % chips
        outgoing = lax.dynamic_index_in_dim(pair_sum, target, 1, False).astype(jnp.bfloat16)
        pairs = [(j, (j + 2 * step) % count) for j in range(count)]
        total = total + lax.ppermute(outgoing, axis, pairs).astype(jnp.float32)
    split = total.reshape(blocks_here, share, width // (2 * block_units), 2, block_units)
    mine = (jax.nn.silu(split[:, :, :, 0]) * split[:, :, :, 1]).astype(jnp.bfloat16)
    mine = mine.reshape(blocks_here, share, width // 2)
    gathered = [mine]
    for step in range(1, chips):
        pairs = [(j, (j + 2 * step) % count) for j in range(count)]
        gathered.append(lax.ppermute(mine, axis, pairs))
    stacked = jnp.stack(gathered, axis=1)
    ordered = jnp.take(stacked, (chip - jnp.arange(chips)) % chips, axis=1)
    other = lax.ppermute(ordered, axis, sibling)
    both = jnp.stack([ordered, other], axis=2)
    full = jnp.take(both, jnp.arange(2) ^ core, axis=2)
    return full.reshape(blocks_here, rows, width // 2)


def per_device(
    tokens,
    queries,
    key_rows,
    values,
    log_decay,
    head_gain,
    expert_gain,
    route_ids,
    route_weight,
    expert_in,
    expert_out,
):
    parity = lax.axis_index("seq") % 2
    partner = [(j, j ^ 1) for j in range(lax.axis_size("seq"))]
    other_in, other_out = lax.ppermute((expert_in, expert_out), "seq", partner)
    length = tokens.shape[0]
    local_width = tokens.shape[1]
    heads_here = log_decay.shape[0]
    head_size = queries.shape[1] // heads_here
    score_scale = head_size ** (-0.5)
    query_heads = queries.reshape(length, heads_here, head_size)
    key_heads = key_rows.reshape(length, heads_here, head_size)
    value_heads = values.reshape(length, heads_here, head_size)
    cumulative = jnp.cumsum(log_decay, axis=1)
    causal = (jnp.arange(length)[:, None] >= jnp.arange(length)[None, :])[None]
    scores = (
        jnp.einsum("thd,shd->hts", query_heads, key_heads, preferred_element_type=jnp.float32)
        * score_scale
    )
    spread = cumulative[:, :, None] - cumulative[:, None, :]
    mixing = jnp.where(causal, scores * jnp.exp(jnp.where(causal, spread, 0.0)), 0.0).astype(
        jnp.bfloat16
    )
    inside = jnp.einsum("hts,shd->thd", mixing, value_heads, preferred_element_type=jnp.float32)
    to_end = jnp.exp(cumulative[:, -1:] - cumulative)
    carried_keys = (key_heads.astype(jnp.float32) * to_end.T[:, :, None]).astype(jnp.bfloat16)
    block_state = jnp.einsum(
        "shd,she->hde", carried_keys, value_heads, preferred_element_type=jnp.float32
    )
    block_decay = jnp.exp(cumulative[:, -1])
    entering = exclusive_scan(block_decay, block_state, "seq")
    entering, other_in, other_out = lax.optimization_barrier((entering, other_in, other_out))
    from_before = jnp.einsum(
        "thd,hde->the",
        query_heads.astype(jnp.float32),
        entering,
        precision=lax.Precision.HIGHEST,
        preferred_element_type=jnp.float32,
    )
    attended = inside + from_before * (jnp.exp(cumulative).T[:, :, None] * score_scale)
    head_rms = lax.rsqrt(jnp.mean(attended * attended, axis=2, keepdims=True) + EPSILON)
    normed_heads = (attended * head_rms).reshape(length, local_width)
    hidden_state = (tokens.astype(jnp.float32) + normed_heads * head_gain).astype(jnp.bfloat16)
    hidden_wide = hidden_state.astype(jnp.float32)
    local_squares = jnp.sum(hidden_wide * hidden_wide, axis=1)
    total_squares = lax.psum(local_squares, "head")
    inverse_rms = lax.rsqrt(total_squares / D + EPSILON)
    expert_input = (hidden_wide * inverse_rms[:, None] * expert_gain).astype(jnp.bfloat16)
    capacity = CAP
    expert_count = EXPERTS
    flat_ids = route_ids.reshape(-1)
    pair_count = flat_ids.shape[0]
    chosen = (flat_ids[:, None] == jnp.arange(expert_count)[None, :]).astype(jnp.float32)
    strictly_before = (jnp.arange(pair_count)[:, None] > jnp.arange(pair_count)[None, :]).astype(
        jnp.float32
    )
    earlier_counts = jnp.dot(
        strictly_before, chosen, precision=lax.Precision.HIGHEST, preferred_element_type=jnp.float32
    )
    slot_index = jnp.sum(earlier_counts * chosen, axis=1).astype(jnp.int32)
    position = (flat_ids * capacity + slot_index).reshape(length, route_ids.shape[1])
    slot_ids = jnp.arange(expert_count * capacity, dtype=jnp.int32)
    picks = position[None, :, :] == slot_ids[:, None, None]
    dispatch_matrix = jnp.any(picks, axis=2).astype(jnp.bfloat16)
    send_rows = jnp.dot(dispatch_matrix, expert_input, preferred_element_type=jnp.float32).astype(
        jnp.bfloat16
    )
    half = capacity // 2
    block_units = expert_out.shape[1]
    send_buffer = send_rows.reshape(expert_count * 2, 1, half, local_width)
    arrived = lax.all_to_all(send_buffer, "seq", split_axis=0, concat_axis=1, tiled=True)
    blocks_here, sources = arrived.shape[0], arrived.shape[1]
    flat_rows = arrived.reshape(blocks_here, sources * half, local_width)
    own_sums = jnp.einsum(
        "erd,edh->erh", flat_rows, expert_in, preferred_element_type=jnp.float32
    ).astype(jnp.bfloat16)
    other_sums = jnp.einsum(
        "erd,edh->erh", flat_rows, other_in, preferred_element_type=jnp.float32
    ).astype(jnp.bfloat16)
    partial_sums = jnp.concatenate([own_sums, other_sums], axis=2)
    activated = head_reduce_activate(partial_sums, "head", block_units)
    activated = activated.reshape(blocks_here, sources * half, 2, block_units)
    first_part = jnp.einsum(
        "erh,ehd->erd", activated[:, :, 0], expert_out, preferred_element_type=jnp.float32
    ).astype(jnp.bfloat16)
    second_part = jnp.einsum(
        "erh,ehd->erd", activated[:, :, 1], other_out, preferred_element_type=jnp.float32
    ).astype(jnp.bfloat16)
    summed = (first_part.astype(jnp.float32) + second_part.astype(jnp.float32)).astype(
        jnp.bfloat16
    )
    summed = summed.reshape(blocks_here, sources, half, local_width)
    returned = lax.all_to_all(summed, "seq", split_axis=1, concat_axis=0, tiled=True)
    merged = returned.reshape(expert_count, capacity, local_width).astype(jnp.float32)
    merged = merged.reshape(expert_count * capacity, local_width)
    slot_rows = merged[position]
    expert_mix = jnp.sum(slot_rows * route_weight[:, :, None], axis=1)
    return (hidden_wide + expert_mix).astype(jnp.bfloat16)


def solution(mesh):
    return jax.shard_map(
        per_device,
        mesh=mesh,
        in_specs=(
            P("seq", "head"),
            P("seq", "head"),
            P("seq", "head"),
            P("seq", "head"),
            P("head", "seq"),
            P("head"),
            P("head"),
            P("seq", None),
            P("seq", None),
            P("seq", "head", None),
            P("seq", None, "head"),
        ),
        out_specs=P("seq", "head"),
        check_vma=False,
    )
```

```python
import jax
import jax.numpy as jnp
from jax import lax
from jax.sharding import PartitionSpec as P

D = 4096
EXPERTS = 32
CAP = 20


EPSILON = 1e-06


def pack_window(decay, state):
    heads, rows, cols = state.shape
    high = decay.astype(jnp.bfloat16)
    low = (decay - high.astype(jnp.float32)).astype(jnp.bfloat16)
    tail = jnp.broadcast_to(jnp.stack([high, low], axis=1)[:, :, None], (heads, 2, cols))
    return jnp.concatenate([state.astype(jnp.bfloat16), tail], axis=1)


def exclusive_scan(decay, state, axis):
    place = lax.axis_index(axis)
    count = lax.axis_size(axis)
    rows = state.shape[1]
    window_decay = decay
    window_state = state
    before_decay = jnp.ones_like(decay)
    before_state = jnp.zeros_like(state)
    shift = 1
    while shift < count:
        pairs = [(j, j + shift) for j in range(count - shift)]
        got = lax.ppermute(pack_window(window_decay, window_state), axis, pairs)
        valid = place >= shift
        got_state = got[:, :rows, :].astype(jnp.float32)
        got_decay = got[:, rows, 0].astype(jnp.float32) + got[:, rows + 1, 0].astype(jnp.float32)
        got_decay = jnp.where(valid, got_decay, 1.0)
        before_state = before_decay[:, None, None] * got_state + before_state
        before_decay = before_decay * got_decay
        window_state = window_decay[:, None, None] * got_state + window_state
        window_decay = window_decay * got_decay
        shift *= 2
    return before_state


def head_reduce_activate(partial, axis, block_units):
    place = lax.axis_index(axis)
    count = lax.axis_size(axis)
    chips = count // 2
    core = place % 2
    chip = place // 2
    blocks_here, rows, width = partial.shape
    share = rows // count
    pieces = partial.reshape(blocks_here, chips, 2, share, width)
    sibling = [(j, j ^ 1) for j in range(count)]
    kept = lax.dynamic_index_in_dim(pieces, core, 2, False).astype(jnp.float32)
    handed = lax.dynamic_index_in_dim(pieces, 1 - core, 2, False)
    pair_sum = kept + lax.ppermute(handed, axis, sibling).astype(jnp.float32)
    total = lax.dynamic_index_in_dim(pair_sum, chip, 1, False)
    for step in range(1, chips):
        target = (chip + step) % chips
        outgoing = lax.dynamic_index_in_dim(pair_sum, target, 1, False).astype(jnp.bfloat16)
        pairs = [(j, (j + 2 * step) % count) for j in range(count)]
        total = total + lax.ppermute(outgoing, axis, pairs).astype(jnp.float32)
    split = total.reshape(blocks_here, share, width // (2 * block_units), 2, block_units)
    mine = (jax.nn.silu(split[:, :, :, 0]) * split[:, :, :, 1]).astype(jnp.bfloat16)
    mine = mine.reshape(blocks_here, share, width // 2)
    gathered = [mine]
    for step in range(1, chips):
        pairs = [(j, (j + 2 * step) % count) for j in range(count)]
        gathered.append(lax.ppermute(mine, axis, pairs))
    stacked = jnp.stack(gathered, axis=1)
    reverse = stacked[:, ::-1]
    doubled = jnp.concatenate([reverse, reverse], axis=1)
    ordered = lax.dynamic_slice_in_dim(doubled, (chips - 1 - chip) % chips, chips, 1)
    other = lax.ppermute(ordered, axis, sibling)
    three = jnp.stack([ordered, other, ordered], axis=2)
    full = lax.dynamic_slice_in_dim(three, core, 2, 2)
    return full.reshape(blocks_here, rows, width // 2)


def per_device(
    tokens,
    queries,
    key_rows,
    values,
    log_decay,
    head_gain,
    expert_gain,
    route_ids,
    route_weight,
    expert_in,
    expert_out,
):
    parity = lax.axis_index("seq") % 2
    partner = [(j, j ^ 1) for j in range(lax.axis_size("seq"))]
    other_in, other_out = lax.ppermute((expert_in, expert_out), "seq", partner)
    length = tokens.shape[0]
    local_width = tokens.shape[1]
    heads_here = log_decay.shape[0]
    head_size = queries.shape[1] // heads_here
    score_scale = head_size ** (-0.5)
    query_heads = queries.reshape(length, heads_here, head_size)
    key_heads = key_rows.reshape(length, heads_here, head_size)
    value_heads = values.reshape(length, heads_here, head_size)
    cumulative = jnp.cumsum(log_decay, axis=1)
    causal = (jnp.arange(length)[:, None] >= jnp.arange(length)[None, :])[None]
    scores = (
        jnp.einsum("thd,shd->hts", query_heads, key_heads, preferred_element_type=jnp.float32)
        * score_scale
    )
    spread = cumulative[:, :, None] - cumulative[:, None, :]
    mixing = jnp.where(causal, scores * jnp.exp(jnp.where(causal, spread, 0.0)), 0.0).astype(
        jnp.bfloat16
    )
    inside = jnp.einsum("hts,shd->thd", mixing, value_heads, preferred_element_type=jnp.float32)
    to_end = jnp.exp(cumulative[:, -1:] - cumulative)
    carried_keys = (key_heads.astype(jnp.float32) * to_end.T[:, :, None]).astype(jnp.bfloat16)
    block_state = jnp.einsum(
        "shd,she->hde", carried_keys, value_heads, preferred_element_type=jnp.float32
    )
    block_decay = jnp.exp(cumulative[:, -1])
    entering = exclusive_scan(block_decay, block_state, "seq")
    entering, other_in, other_out = lax.optimization_barrier((entering, other_in, other_out))
    from_before = jnp.einsum(
        "thd,hde->the",
        query_heads.astype(jnp.float32),
        entering,
        precision=lax.Precision.HIGHEST,
        preferred_element_type=jnp.float32,
    )
    attended = inside + from_before * (jnp.exp(cumulative).T[:, :, None] * score_scale)
    head_rms = lax.rsqrt(jnp.mean(attended * attended, axis=2, keepdims=True) + EPSILON)
    normed_heads = (attended * head_rms).reshape(length, local_width)
    hidden_state = (tokens.astype(jnp.float32) + normed_heads * head_gain).astype(jnp.bfloat16)
    hidden_wide = hidden_state.astype(jnp.float32)
    local_squares = jnp.sum(hidden_wide * hidden_wide, axis=1)
    total_squares = lax.psum(local_squares, "head")
    inverse_rms = lax.rsqrt(total_squares / D + EPSILON)
    expert_input = (hidden_wide * inverse_rms[:, None] * expert_gain).astype(jnp.bfloat16)
    capacity = CAP
    expert_count = EXPERTS
    flat_ids = route_ids.reshape(-1)
    pair_count = flat_ids.shape[0]
    chosen = (flat_ids[:, None] == jnp.arange(expert_count)[None, :]).astype(jnp.float32)
    strictly_before = (jnp.arange(pair_count)[:, None] > jnp.arange(pair_count)[None, :]).astype(
        jnp.float32
    )
    earlier_counts = jnp.dot(
        strictly_before, chosen, precision=lax.Precision.HIGHEST, preferred_element_type=jnp.float32
    )
    slot_index = jnp.sum(earlier_counts * chosen, axis=1).astype(jnp.int32)
    position = (flat_ids * capacity + slot_index).reshape(length, route_ids.shape[1])
    slot_ids = jnp.arange(expert_count * capacity, dtype=jnp.int32)
    picks = position[None, :, :] == slot_ids[:, None, None]
    dispatch_matrix = jnp.any(picks, axis=2).astype(jnp.bfloat16)
    send_rows = jnp.dot(dispatch_matrix, expert_input, preferred_element_type=jnp.float32).astype(
        jnp.bfloat16
    )
    half = capacity // 2
    block_units = expert_out.shape[1]
    send_buffer = send_rows.reshape(expert_count * 2, 1, half, local_width)
    arrived = lax.all_to_all(send_buffer, "seq", split_axis=0, concat_axis=1, tiled=True)
    blocks_here, sources = arrived.shape[0], arrived.shape[1]
    flat_rows = arrived.reshape(blocks_here, sources * half, local_width)
    own_sums = jnp.einsum(
        "erd,edh->erh", flat_rows, expert_in, preferred_element_type=jnp.float32
    ).astype(jnp.bfloat16)
    other_sums = jnp.einsum(
        "erd,edh->erh", flat_rows, other_in, preferred_element_type=jnp.float32
    ).astype(jnp.bfloat16)
    partial_sums = jnp.concatenate([own_sums, other_sums], axis=2)
    activated = head_reduce_activate(partial_sums, "head", block_units)
    activated = activated.reshape(blocks_here, sources * half, 2, block_units)
    weight_out = jnp.stack([expert_out, other_out], axis=1)
    summed = jnp.einsum(
        "erkh,ekhd->erd", activated, weight_out, preferred_element_type=jnp.float32
    ).astype(jnp.bfloat16)
    summed = summed.reshape(blocks_here, sources, half, local_width)
    returned = lax.all_to_all(summed, "seq", split_axis=1, concat_axis=0, tiled=True)
    merged = returned.reshape(expert_count, capacity, local_width).astype(jnp.float32)
    merged = merged.reshape(expert_count * capacity, local_width)
    slot_rows = merged[position]
    expert_mix = jnp.sum(slot_rows * route_weight[:, :, None], axis=1)
    return (hidden_wide + expert_mix).astype(jnp.bfloat16)


def solution(mesh):
    return jax.shard_map(
        per_device,
        mesh=mesh,
        in_specs=(
            P("seq", "head"),
            P("seq", "head"),
            P("seq", "head"),
            P("seq", "head"),
            P("head", "seq"),
            P("head"),
            P("head"),
            P("seq", None),
            P("seq", None),
            P("seq", "head", None),
            P("seq", None, "head"),
        ),
        out_specs=P("seq", "head"),
        check_vma=False,
    )
```

```python
import jax
import jax.numpy as jnp
from jax import lax
from jax.sharding import PartitionSpec as P

D = 4096
EXPERTS = 32
CAP = 20


EPSILON = 1e-06


def pack_window(decay, state):
    heads, rows, cols = state.shape
    high = decay.astype(jnp.bfloat16)
    low = (decay - high.astype(jnp.float32)).astype(jnp.bfloat16)
    tail = jnp.broadcast_to(jnp.stack([high, low], axis=1)[:, :, None], (heads, 2, cols))
    return jnp.concatenate([state.astype(jnp.bfloat16), tail], axis=1)


def exclusive_scan(decay, state, axis):
    place = lax.axis_index(axis)
    count = lax.axis_size(axis)
    rows = state.shape[1]
    window_decay = decay
    window_state = state
    before_decay = jnp.ones_like(decay)
    before_state = jnp.zeros_like(state)
    shift = 1
    while shift < count:
        pairs = [(j, j + shift) for j in range(count - shift)]
        got = lax.ppermute(pack_window(window_decay, window_state), axis, pairs)
        valid = place >= shift
        got_state = got[:, :rows, :].astype(jnp.float32)
        got_decay = got[:, rows, 0].astype(jnp.float32) + got[:, rows + 1, 0].astype(jnp.float32)
        got_decay = jnp.where(valid, got_decay, 1.0)
        before_state = before_decay[:, None, None] * got_state + before_state
        before_decay = before_decay * got_decay
        window_state = window_decay[:, None, None] * got_state + window_state
        window_decay = window_decay * got_decay
        shift *= 2
    return before_state


def head_reduce_activate(partial, axis, block_units):
    place = lax.axis_index(axis)
    count = lax.axis_size(axis)
    chips = count // 2
    core = place % 2
    chip = place // 2
    blocks_here, rows, width = partial.shape
    share = rows // count
    pieces = partial.reshape(blocks_here, chips, 2, share, width)
    sibling = [(j, j ^ 1) for j in range(count)]
    kept = lax.dynamic_index_in_dim(pieces, core, 2, False).astype(jnp.float32)
    handed = lax.dynamic_index_in_dim(pieces, 1 - core, 2, False)
    pair_sum = kept + lax.ppermute(handed, axis, sibling).astype(jnp.float32)
    total = lax.dynamic_index_in_dim(pair_sum, chip, 1, False)
    for step in range(1, chips):
        target = (chip + step) % chips
        outgoing = lax.dynamic_index_in_dim(pair_sum, target, 1, False).astype(jnp.bfloat16)
        pairs = [(j, (j + 2 * step) % count) for j in range(count)]
        total = total + lax.ppermute(outgoing, axis, pairs).astype(jnp.float32)
    split = total.reshape(blocks_here, share, width // (2 * block_units), 2, block_units)
    mine = (jax.nn.silu(split[:, :, :, 0]) * split[:, :, :, 1]).astype(jnp.bfloat16)
    mine = mine.reshape(blocks_here, share, width // 2)
    gathered = [mine]
    for step in range(1, chips):
        pairs = [(j, (j + 2 * step) % count) for j in range(count)]
        gathered.append(lax.ppermute(mine, axis, pairs))
    stacked = jnp.stack(gathered, axis=1)
    reverse = stacked[:, ::-1]
    doubled = jnp.concatenate([reverse, reverse], axis=1)
    ordered = lax.dynamic_slice_in_dim(doubled, (chips - 1 - chip) % chips, chips, 1)
    other = lax.ppermute(ordered, axis, sibling)
    three = jnp.stack([ordered, other, ordered], axis=2)
    full = lax.dynamic_slice_in_dim(three, core, 2, 2)
    return full.reshape(blocks_here, rows, width // 2)


def per_device(
    tokens,
    queries,
    key_rows,
    values,
    log_decay,
    head_gain,
    expert_gain,
    route_ids,
    route_weight,
    expert_in,
    expert_out,
):
    parity = lax.axis_index("seq") % 2
    partner = [(j, j ^ 1) for j in range(lax.axis_size("seq"))]
    other_in = lax.ppermute(expert_in, "seq", partner)
    other_out = lax.ppermute(expert_out, "seq", partner)
    length = tokens.shape[0]
    local_width = tokens.shape[1]
    heads_here = log_decay.shape[0]
    head_size = queries.shape[1] // heads_here
    score_scale = head_size ** (-0.5)
    query_heads = queries.reshape(length, heads_here, head_size)
    key_heads = key_rows.reshape(length, heads_here, head_size)
    value_heads = values.reshape(length, heads_here, head_size)
    cumulative = jnp.cumsum(log_decay, axis=1)
    causal = (jnp.arange(length)[:, None] >= jnp.arange(length)[None, :])[None]
    scores = (
        jnp.einsum("thd,shd->hts", query_heads, key_heads, preferred_element_type=jnp.float32)
        * score_scale
    )
    spread = cumulative[:, :, None] - cumulative[:, None, :]
    mixing = jnp.where(causal, scores * jnp.exp(jnp.where(causal, spread, 0.0)), 0.0).astype(
        jnp.bfloat16
    )
    inside = jnp.einsum("hts,shd->thd", mixing, value_heads, preferred_element_type=jnp.float32)
    to_end = jnp.exp(cumulative[:, -1:] - cumulative)
    carried_keys = (key_heads.astype(jnp.float32) * to_end.T[:, :, None]).astype(jnp.bfloat16)
    block_state = jnp.einsum(
        "shd,she->hde", carried_keys, value_heads, preferred_element_type=jnp.float32
    )
    block_decay = jnp.exp(cumulative[:, -1])
    entering = exclusive_scan(block_decay, block_state, "seq")
    entering, other_in = lax.optimization_barrier((entering, other_in))
    from_before = jnp.einsum(
        "thd,hde->the",
        query_heads.astype(jnp.float32),
        entering,
        precision=lax.Precision.HIGHEST,
        preferred_element_type=jnp.float32,
    )
    attended = inside + from_before * (jnp.exp(cumulative).T[:, :, None] * score_scale)
    head_rms = lax.rsqrt(jnp.mean(attended * attended, axis=2, keepdims=True) + EPSILON)
    normed_heads = (attended * head_rms).reshape(length, local_width)
    hidden_state = (tokens.astype(jnp.float32) + normed_heads * head_gain).astype(jnp.bfloat16)
    hidden_wide = hidden_state.astype(jnp.float32)
    local_squares = jnp.sum(hidden_wide * hidden_wide, axis=1)
    total_squares = lax.psum(local_squares, "head")
    inverse_rms = lax.rsqrt(total_squares / D + EPSILON)
    expert_input = (hidden_wide * inverse_rms[:, None] * expert_gain).astype(jnp.bfloat16)
    capacity = CAP
    expert_count = EXPERTS
    flat_ids = route_ids.reshape(-1)
    pair_count = flat_ids.shape[0]
    chosen = (flat_ids[:, None] == jnp.arange(expert_count)[None, :]).astype(jnp.float32)
    strictly_before = (jnp.arange(pair_count)[:, None] > jnp.arange(pair_count)[None, :]).astype(
        jnp.float32
    )
    earlier_counts = jnp.dot(
        strictly_before, chosen, precision=lax.Precision.HIGHEST, preferred_element_type=jnp.float32
    )
    slot_index = jnp.sum(earlier_counts * chosen, axis=1).astype(jnp.int32)
    position = (flat_ids * capacity + slot_index).reshape(length, route_ids.shape[1])
    slot_ids = jnp.arange(expert_count * capacity, dtype=jnp.int32)
    picks = position[None, :, :] == slot_ids[:, None, None]
    dispatch_matrix = jnp.any(picks, axis=2).astype(jnp.bfloat16)
    send_rows = jnp.dot(dispatch_matrix, expert_input, preferred_element_type=jnp.float32).astype(
        jnp.bfloat16
    )
    half = capacity // 2
    block_units = expert_out.shape[1]
    send_buffer = send_rows.reshape(expert_count * 2, 1, half, local_width)
    arrived = lax.all_to_all(send_buffer, "seq", split_axis=0, concat_axis=1, tiled=True)
    blocks_here, sources = arrived.shape[0], arrived.shape[1]
    arrived, other_out = lax.optimization_barrier((arrived, other_out))
    flat_rows = arrived.reshape(blocks_here, sources * half, local_width)
    own_sums = jnp.einsum(
        "erd,edh->erh", flat_rows, expert_in, preferred_element_type=jnp.float32
    ).astype(jnp.bfloat16)
    other_sums = jnp.einsum(
        "erd,edh->erh", flat_rows, other_in, preferred_element_type=jnp.float32
    ).astype(jnp.bfloat16)
    partial_sums = jnp.concatenate([own_sums, other_sums], axis=2)
    activated = head_reduce_activate(partial_sums, "head", block_units)
    activated = activated.reshape(blocks_here, sources * half, 2, block_units)
    weight_out = jnp.stack([expert_out, other_out], axis=1)
    summed = jnp.einsum(
        "erkh,ekhd->erd", activated, weight_out, preferred_element_type=jnp.float32
    ).astype(jnp.bfloat16)
    summed = summed.reshape(blocks_here, sources, half, local_width)
    returned = lax.all_to_all(summed, "seq", split_axis=1, concat_axis=0, tiled=True)
    merged = returned.reshape(expert_count, capacity, local_width).astype(jnp.float32)
    merged = merged.reshape(expert_count * capacity, local_width)
    slot_rows = merged[position]
    expert_mix = jnp.sum(slot_rows * route_weight[:, :, None], axis=1)
    return (hidden_wide + expert_mix).astype(jnp.bfloat16)


def solution(mesh):
    return jax.shard_map(
        per_device,
        mesh=mesh,
        in_specs=(
            P("seq", "head"),
            P("seq", "head"),
            P("seq", "head"),
            P("seq", "head"),
            P("head", "seq"),
            P("head"),
            P("head"),
            P("seq", None),
            P("seq", None),
            P("seq", "head", None),
            P("seq", None, "head"),
        ),
        out_specs=P("seq", "head"),
        check_vma=False,
    )
```

```python
import jax
import jax.numpy as jnp
from jax import lax
from jax.sharding import PartitionSpec as P

D = 4096
EXPERTS = 32
CAP = 20


EPSILON = 1e-06


def pack_window(decay, state):
    heads, rows, cols = state.shape
    high = decay.astype(jnp.bfloat16)
    low = (decay - high.astype(jnp.float32)).astype(jnp.bfloat16)
    tail = jnp.broadcast_to(jnp.stack([high, low], axis=1)[:, :, None], (heads, 2, cols))
    return jnp.concatenate([state.astype(jnp.bfloat16), tail], axis=1)


def exclusive_scan(decay, state, axis):
    place = lax.axis_index(axis)
    count = lax.axis_size(axis)
    rows = state.shape[1]
    window_decay = decay
    window_state = state
    before_decay = jnp.ones_like(decay)
    before_state = jnp.zeros_like(state)
    shift = 1
    while shift < count:
        pairs = [(j, j + shift) for j in range(count - shift)]
        got = lax.ppermute(pack_window(window_decay, window_state), axis, pairs)
        valid = place >= shift
        got_state = got[:, :rows, :].astype(jnp.float32)
        got_decay = got[:, rows, 0].astype(jnp.float32) + got[:, rows + 1, 0].astype(jnp.float32)
        got_decay = jnp.where(valid, got_decay, 1.0)
        before_state = before_decay[:, None, None] * got_state + before_state
        before_decay = before_decay * got_decay
        window_state = window_decay[:, None, None] * got_state + window_state
        window_decay = window_decay * got_decay
        shift *= 2
    return before_state


def head_reduce_activate(partial, axis, block_units):
    place = lax.axis_index(axis)
    count = lax.axis_size(axis)
    chips = count // 2
    core = place % 2
    chip = place // 2
    blocks_here, rows, width = partial.shape
    share = rows // count
    pieces = partial.reshape(blocks_here, chips, 2, share, width)
    sibling = [(j, j ^ 1) for j in range(count)]
    kept = lax.dynamic_index_in_dim(pieces, core, 2, False).astype(jnp.float32)
    handed = lax.dynamic_index_in_dim(pieces, 1 - core, 2, False)
    pair_sum = kept + lax.ppermute(handed, axis, sibling).astype(jnp.float32)
    total = lax.dynamic_index_in_dim(pair_sum, chip, 1, False)
    for step in range(1, chips):
        target = (chip + step) % chips
        outgoing = lax.dynamic_index_in_dim(pair_sum, target, 1, False).astype(jnp.bfloat16)
        pairs = [(j, (j + 2 * step) % count) for j in range(count)]
        total = total + lax.ppermute(outgoing, axis, pairs).astype(jnp.float32)
    split = total.reshape(blocks_here, share, width // (2 * block_units), 2, block_units)
    mine = (jax.nn.silu(split[:, :, :, 0]) * split[:, :, :, 1]).astype(jnp.bfloat16)
    mine = mine.reshape(blocks_here, share, width // 2)
    gathered = [mine]
    for step in range(1, chips):
        pairs = [(j, (j + 2 * step) % count) for j in range(count)]
        gathered.append(lax.ppermute(mine, axis, pairs))
    stacked = jnp.stack(gathered, axis=1)
    reverse = stacked[:, ::-1]
    doubled = jnp.concatenate([reverse, reverse], axis=1)
    ordered = lax.dynamic_slice_in_dim(doubled, (chips - 1 - chip) % chips, chips, 1)
    other = lax.ppermute(ordered, axis, sibling)
    three = jnp.stack([ordered, other, ordered], axis=2)
    full = lax.dynamic_slice_in_dim(three, core, 2, 2)
    return full.reshape(blocks_here, rows, width // 2)


def per_device(
    tokens,
    queries,
    key_rows,
    values,
    log_decay,
    head_gain,
    expert_gain,
    route_ids,
    route_weight,
    expert_in,
    expert_out,
):
    parity = lax.axis_index("seq") % 2
    partner = [(j, j ^ 1) for j in range(lax.axis_size("seq"))]
    other_in = lax.ppermute(expert_in, "seq", partner)
    other_out = lax.ppermute(expert_out, "seq", partner)
    length = tokens.shape[0]
    local_width = tokens.shape[1]
    heads_here = log_decay.shape[0]
    head_size = queries.shape[1] // heads_here
    score_scale = head_size ** (-0.5)
    query_heads = queries.reshape(length, heads_here, head_size)
    key_heads = key_rows.reshape(length, heads_here, head_size)
    value_heads = values.reshape(length, heads_here, head_size)
    cumulative = jnp.cumsum(log_decay, axis=1)
    causal = (jnp.arange(length)[:, None] >= jnp.arange(length)[None, :])[None]
    scores = (
        jnp.einsum("thd,shd->hts", query_heads, key_heads, preferred_element_type=jnp.float32)
        * score_scale
    )
    spread = cumulative[:, :, None] - cumulative[:, None, :]
    mixing = jnp.where(causal, scores * jnp.exp(jnp.where(causal, spread, 0.0)), 0.0).astype(
        jnp.bfloat16
    )
    inside = jnp.einsum("hts,shd->thd", mixing, value_heads, preferred_element_type=jnp.float32)
    to_end = jnp.exp(cumulative[:, -1:] - cumulative)
    carried_keys = (key_heads.astype(jnp.float32) * to_end.T[:, :, None]).astype(jnp.bfloat16)
    block_state = jnp.einsum(
        "shd,she->hde", carried_keys, value_heads, preferred_element_type=jnp.float32
    )
    block_decay = jnp.exp(cumulative[:, -1])
    entering = exclusive_scan(block_decay, block_state, "seq")
    entering, other_in = lax.optimization_barrier((entering, other_in))
    from_before = jnp.einsum(
        "thd,hde->the",
        query_heads.astype(jnp.float32),
        entering,
        precision=lax.Precision.HIGHEST,
        preferred_element_type=jnp.float32,
    )
    attended = inside + from_before * (jnp.exp(cumulative).T[:, :, None] * score_scale)
    head_rms = lax.rsqrt(jnp.mean(attended * attended, axis=2, keepdims=True) + EPSILON)
    normed_heads = (attended * head_rms).reshape(length, local_width)
    hidden_state = (tokens.astype(jnp.float32) + normed_heads * head_gain).astype(jnp.bfloat16)
    hidden_wide = hidden_state.astype(jnp.float32)
    local_squares = jnp.sum(hidden_wide * hidden_wide, axis=1)
    total_squares = lax.psum(local_squares, "head")
    inverse_rms = lax.rsqrt(total_squares / D + EPSILON)
    expert_input = (hidden_wide * inverse_rms[:, None] * expert_gain).astype(jnp.bfloat16)
    capacity = CAP
    expert_count = EXPERTS
    flat_ids = route_ids.reshape(-1)
    pair_count = flat_ids.shape[0]
    chosen = (flat_ids[:, None] == jnp.arange(expert_count)[None, :]).astype(jnp.float32)
    strictly_before = (jnp.arange(pair_count)[:, None] > jnp.arange(pair_count)[None, :]).astype(
        jnp.float32
    )
    earlier_counts = jnp.dot(
        strictly_before, chosen, precision=lax.Precision.HIGHEST, preferred_element_type=jnp.float32
    )
    slot_index = jnp.sum(earlier_counts * chosen, axis=1).astype(jnp.int32)
    position = (flat_ids * capacity + slot_index).reshape(length, route_ids.shape[1])
    slot_ids = jnp.arange(expert_count * capacity, dtype=jnp.int32)
    picks = position[None, :, :] == slot_ids[:, None, None]
    dispatch_matrix = jnp.any(picks, axis=2).astype(jnp.bfloat16)
    send_rows = jnp.dot(dispatch_matrix, expert_input, preferred_element_type=jnp.float32).astype(
        jnp.bfloat16
    )
    half = capacity // 2
    block_units = expert_out.shape[1]
    send_buffer = send_rows.reshape(expert_count * 2, 1, half, local_width)
    arrived = lax.all_to_all(send_buffer, "seq", split_axis=0, concat_axis=1, tiled=True)
    blocks_here, sources = arrived.shape[0], arrived.shape[1]
    flat_rows = arrived.reshape(blocks_here, sources * half, local_width)
    own_sums = jnp.einsum(
        "erd,edh->erh", flat_rows, expert_in, preferred_element_type=jnp.float32
    ).astype(jnp.bfloat16)
    other_sums = jnp.einsum(
        "erd,edh->erh", flat_rows, other_in, preferred_element_type=jnp.float32
    ).astype(jnp.bfloat16)
    partial_sums = jnp.concatenate([own_sums, other_sums], axis=2)
    activated = head_reduce_activate(partial_sums, "head", block_units)
    activated, other_out = lax.optimization_barrier((activated, other_out))
    activated = activated.reshape(blocks_here, sources * half, 2, block_units)
    weight_out = jnp.stack([expert_out, other_out], axis=1)
    summed = jnp.einsum(
        "erkh,ekhd->erd", activated, weight_out, preferred_element_type=jnp.float32
    ).astype(jnp.bfloat16)
    summed = summed.reshape(blocks_here, sources, half, local_width)
    returned = lax.all_to_all(summed, "seq", split_axis=1, concat_axis=0, tiled=True)
    merged = returned.reshape(expert_count, capacity, local_width).astype(jnp.float32)
    merged = merged.reshape(expert_count * capacity, local_width)
    slot_rows = merged[position]
    expert_mix = jnp.sum(slot_rows * route_weight[:, :, None], axis=1)
    return (hidden_wide + expert_mix).astype(jnp.bfloat16)


def solution(mesh):
    return jax.shard_map(
        per_device,
        mesh=mesh,
        in_specs=(
            P("seq", "head"),
            P("seq", "head"),
            P("seq", "head"),
            P("seq", "head"),
            P("head", "seq"),
            P("head"),
            P("head"),
            P("seq", None),
            P("seq", None),
            P("seq", "head", None),
            P("seq", None, "head"),
        ),
        out_specs=P("seq", "head"),
        check_vma=False,
    )
```

```python
import jax
import jax.numpy as jnp
from jax import lax
from jax.sharding import PartitionSpec as P

D = 4096
EXPERTS = 32
CAP = 20


EPSILON = 1e-06


def pack_window(decay, state):
    heads, rows, cols = state.shape
    high = decay.astype(jnp.bfloat16)
    low = (decay - high.astype(jnp.float32)).astype(jnp.bfloat16)
    tail = jnp.broadcast_to(jnp.stack([high, low], axis=1)[:, :, None], (heads, 2, cols))
    return jnp.concatenate([state.astype(jnp.bfloat16), tail], axis=1)


def exclusive_scan(decay, state, axis):
    place = lax.axis_index(axis)
    count = lax.axis_size(axis)
    rows = state.shape[1]
    window_decay = decay
    window_state = state
    before_decay = jnp.ones_like(decay)
    before_state = jnp.zeros_like(state)
    shift = 1
    while shift < count:
        pairs = [(j, j + shift) for j in range(count - shift)]
        got = lax.ppermute(pack_window(window_decay, window_state), axis, pairs)
        valid = place >= shift
        got_state = got[:, :rows, :].astype(jnp.float32)
        got_decay = got[:, rows, 0].astype(jnp.float32) + got[:, rows + 1, 0].astype(jnp.float32)
        got_decay = jnp.where(valid, got_decay, 1.0)
        before_state = before_decay[:, None, None] * got_state + before_state
        before_decay = before_decay * got_decay
        window_state = window_decay[:, None, None] * got_state + window_state
        window_decay = window_decay * got_decay
        shift *= 2
    return before_state


def head_reduce_activate(partial, axis, block_units):
    place = lax.axis_index(axis)
    count = lax.axis_size(axis)
    chips = count // 2
    core = place % 2
    chip = place // 2
    blocks_here, rows, width = partial.shape
    share = rows // count
    pieces = partial.reshape(blocks_here, chips, 2, share, width)
    sibling = [(j, j ^ 1) for j in range(count)]
    kept = lax.dynamic_index_in_dim(pieces, core, 2, False).astype(jnp.float32)
    handed = lax.dynamic_index_in_dim(pieces, 1 - core, 2, False)
    pair_sum = kept + lax.ppermute(handed, axis, sibling).astype(jnp.float32)
    total = lax.dynamic_index_in_dim(pair_sum, chip, 1, False)
    for step in range(1, chips):
        target = (chip + step) % chips
        outgoing = lax.dynamic_index_in_dim(pair_sum, target, 1, False).astype(jnp.bfloat16)
        pairs = [(j, (j + 2 * step) % count) for j in range(count)]
        total = total + lax.ppermute(outgoing, axis, pairs).astype(jnp.float32)
    split = total.reshape(blocks_here, share, width // (2 * block_units), 2, block_units)
    mine = (jax.nn.silu(split[:, :, :, 0]) * split[:, :, :, 1]).astype(jnp.bfloat16)
    mine = mine.reshape(blocks_here, share, width // 2)
    gathered = [mine]
    for step in range(1, chips):
        pairs = [(j, (j + 2 * step) % count) for j in range(count)]
        gathered.append(lax.ppermute(mine, axis, pairs))
    stacked = jnp.stack(gathered, axis=1)
    reverse = stacked[:, ::-1]
    doubled = jnp.concatenate([reverse, reverse], axis=1)
    ordered = lax.dynamic_slice_in_dim(doubled, (chips - 1 - chip) % chips, chips, 1)
    other = lax.ppermute(ordered, axis, sibling)
    three = jnp.stack([ordered, other, ordered], axis=2)
    full = lax.dynamic_slice_in_dim(three, core, 2, 2)
    return full.reshape(blocks_here, rows, width // 2)


def per_device(
    tokens,
    queries,
    key_rows,
    values,
    log_decay,
    head_gain,
    expert_gain,
    route_ids,
    route_weight,
    expert_in,
    expert_out,
):
    parity = lax.axis_index("seq") % 2
    partner = [(j, j ^ 1) for j in range(lax.axis_size("seq"))]
    other_in = lax.ppermute(expert_in, "seq", partner)
    other_out = lax.ppermute(expert_out, "seq", partner)
    length = tokens.shape[0]
    local_width = tokens.shape[1]
    heads_here = log_decay.shape[0]
    head_size = queries.shape[1] // heads_here
    score_scale = head_size ** (-0.5)
    query_heads = queries.reshape(length, heads_here, head_size)
    key_heads = key_rows.reshape(length, heads_here, head_size)
    value_heads = values.reshape(length, heads_here, head_size)
    cumulative = jnp.cumsum(log_decay, axis=1)
    causal = (jnp.arange(length)[:, None] >= jnp.arange(length)[None, :])[None]
    scores = (
        jnp.einsum("thd,shd->hts", query_heads, key_heads, preferred_element_type=jnp.float32)
        * score_scale
    )
    spread = cumulative[:, :, None] - cumulative[:, None, :]
    mixing = jnp.where(causal, scores * jnp.exp(jnp.where(causal, spread, 0.0)), 0.0).astype(
        jnp.bfloat16
    )
    inside = jnp.einsum("hts,shd->thd", mixing, value_heads, preferred_element_type=jnp.float32)
    to_end = jnp.exp(cumulative[:, -1:] - cumulative)
    carried_keys = (key_heads.astype(jnp.float32) * to_end.T[:, :, None]).astype(jnp.bfloat16)
    block_state = jnp.einsum(
        "shd,she->hde", carried_keys, value_heads, preferred_element_type=jnp.float32
    )
    block_decay = jnp.exp(cumulative[:, -1])
    entering = exclusive_scan(block_decay, block_state, "seq")
    from_before = jnp.einsum(
        "thd,hde->the",
        query_heads.astype(jnp.float32),
        entering,
        precision=lax.Precision.HIGHEST,
        preferred_element_type=jnp.float32,
    )
    attended = inside + from_before * (jnp.exp(cumulative).T[:, :, None] * score_scale)
    head_rms = lax.rsqrt(jnp.mean(attended * attended, axis=2, keepdims=True) + EPSILON)
    normed_heads = (attended * head_rms).reshape(length, local_width)
    hidden_state = (tokens.astype(jnp.float32) + normed_heads * head_gain).astype(jnp.bfloat16)
    hidden_wide = hidden_state.astype(jnp.float32)
    local_squares = jnp.sum(hidden_wide * hidden_wide, axis=1)
    total_squares = lax.psum(local_squares, "head")
    total_squares, other_in = lax.optimization_barrier((total_squares, other_in))
    inverse_rms = lax.rsqrt(total_squares / D + EPSILON)
    expert_input = (hidden_wide * inverse_rms[:, None] * expert_gain).astype(jnp.bfloat16)
    capacity = CAP
    expert_count = EXPERTS
    flat_ids = route_ids.reshape(-1)
    pair_count = flat_ids.shape[0]
    chosen = (flat_ids[:, None] == jnp.arange(expert_count)[None, :]).astype(jnp.float32)
    strictly_before = (jnp.arange(pair_count)[:, None] > jnp.arange(pair_count)[None, :]).astype(
        jnp.float32
    )
    earlier_counts = jnp.dot(
        strictly_before, chosen, precision=lax.Precision.HIGHEST, preferred_element_type=jnp.float32
    )
    slot_index = jnp.sum(earlier_counts * chosen, axis=1).astype(jnp.int32)
    position = (flat_ids * capacity + slot_index).reshape(length, route_ids.shape[1])
    slot_ids = jnp.arange(expert_count * capacity, dtype=jnp.int32)
    picks = position[None, :, :] == slot_ids[:, None, None]
    dispatch_matrix = jnp.any(picks, axis=2).astype(jnp.bfloat16)
    send_rows = jnp.dot(dispatch_matrix, expert_input, preferred_element_type=jnp.float32).astype(
        jnp.bfloat16
    )
    half = capacity // 2
    block_units = expert_out.shape[1]
    send_buffer = send_rows.reshape(expert_count * 2, 1, half, local_width)
    arrived = lax.all_to_all(send_buffer, "seq", split_axis=0, concat_axis=1, tiled=True)
    blocks_here, sources = arrived.shape[0], arrived.shape[1]
    flat_rows = arrived.reshape(blocks_here, sources * half, local_width)
    own_sums = jnp.einsum(
        "erd,edh->erh", flat_rows, expert_in, preferred_element_type=jnp.float32
    ).astype(jnp.bfloat16)
    other_sums = jnp.einsum(
        "erd,edh->erh", flat_rows, other_in, preferred_element_type=jnp.float32
    ).astype(jnp.bfloat16)
    partial_sums = jnp.concatenate([own_sums, other_sums], axis=2)
    activated = head_reduce_activate(partial_sums, "head", block_units)
    activated, other_out = lax.optimization_barrier((activated, other_out))
    activated = activated.reshape(blocks_here, sources * half, 2, block_units)
    weight_out = jnp.stack([expert_out, other_out], axis=1)
    summed = jnp.einsum(
        "erkh,ekhd->erd", activated, weight_out, preferred_element_type=jnp.float32
    ).astype(jnp.bfloat16)
    summed = summed.reshape(blocks_here, sources, half, local_width)
    returned = lax.all_to_all(summed, "seq", split_axis=1, concat_axis=0, tiled=True)
    merged = returned.reshape(expert_count, capacity, local_width).astype(jnp.float32)
    merged = merged.reshape(expert_count * capacity, local_width)
    slot_rows = merged[position]
    expert_mix = jnp.sum(slot_rows * route_weight[:, :, None], axis=1)
    return (hidden_wide + expert_mix).astype(jnp.bfloat16)


def solution(mesh):
    return jax.shard_map(
        per_device,
        mesh=mesh,
        in_specs=(
            P("seq", "head"),
            P("seq", "head"),
            P("seq", "head"),
            P("seq", "head"),
            P("head", "seq"),
            P("head"),
            P("head"),
            P("seq", None),
            P("seq", None),
            P("seq", "head", None),
            P("seq", None, "head"),
        ),
        out_specs=P("seq", "head"),
        check_vma=False,
    )
```
